256 devices in a mesh: ctx: 64 (over y, z, core), ch: 4 (over x).
Axes of the slice: x: 4, y: 4, z: 8, core: 2. Of those that a mesh axis runs over, the one named last changes fastest.
Arguments:
- stream: bfloat16 [8192, 4096], P('ctx', 'ch'), may hold values from -6 to 6
- norm_gain: float32 [4096], P('ch'), may hold values from 0.25 to 1.75
- short_filters: float32 [3, 3, 4096], P(None, None, 'ch'), may hold values from -3.5 to 3.5
- mode_rates: float32 [16, 4096], P(None, 'ch'), as said below
- residues: float32 [16, 4096], P(None, 'ch'), as said below
- grad_out: bfloat16 [8192, 4096], P('ctx', 'ch'), may hold values from -6 to 6
Outputs:
- output: bfloat16 [8192, 4096], P('ctx', 'ch')
- grad_stream: bfloat16 [8192, 4096], P('ctx', 'ch')
- grad_residues: float32 [16, 4096], P(None, 'ch')
- grad_short: float32 [3, 3, 4096], P(None, None, 'ch')
The draws below stay inside these ranges and needn't reach their ends.
Inputs may be any that keep to these rules, and one draw needn't show every extreme that they name: `mode_rates`: each rate lies between 0.05 / 8192 and 0.03. `residues`: each weight is at most 4 * sqrt(0.06 / 16) in magnitude.
All inputs are finite; a program needn't handle non-finite values.
Results may differ from the reference program's by a relative error of at most 0.0054.
Values may be sent and summed in bfloat16 or wider, within the bound.
No kernel may reach another device: no remote copies, remote signals or barrier semaphores. Data moves between devices by JAX's collectives and lax.ppermute only.
A program may use at most 192 MiB of HBM per device.

```python
from functools import partial
import jax
import jax.numpy as jnp
from jax import lax

CH = 4096
M = 16
KS = 3
P_SIZE = 32
TOKENS = 8192


def rate_draw(key, share):
    first, second, third = jax.random.split(jax.random.fold_in(key, 7), 3)
    chosen = jax.random.bernoulli(first, share, (M, CH))
    slow_rates = jnp.exp(jax.random.uniform(second, (M, CH), jnp.float32, jnp.log(0.05 / TOKENS), jnp.log(2.0 / TOKENS)))
    fast_rates = jnp.exp(jax.random.uniform(third, (M, CH), jnp.float32, jnp.log(4.0 / TOKENS), jnp.log(0.03)))
    return jnp.where(chosen, slow_rates, fast_rates)


def draw_mode_rates(key, part):
    share = 0.5
    return rate_draw(key, share)


def draw_residues(key, part):
    noise_key = jax.random.fold_in(key, 8)
    share = 0.5
    noise = jnp.clip(jax.random.normal(noise_key, (M, CH), jnp.float32), -4.0, 4.0)
    decay_rates = rate_draw(key, share)
    return noise * jnp.sqrt(2.0 * jnp.maximum(decay_rates, 1.0 / TOKENS) / M)


def shard_levels(stream_key, dims, pieces, low, high):
    gain, own = 1.0, jax.random.fold_in(stream_key, 6)
    for position, blocks in pieces:
        heights = jnp.exp(jax.random.uniform(jax.random.fold_in(own, position), (blocks,), jnp.float32, low / len(pieces), high / len(pieces)))
        gain = gain * jnp.repeat(heights, dims[position] // blocks).reshape([-1 if axis == position else 1 for axis in range(len(dims))])
    return gain


def gaussian(own_key, dims, spread, bound, cuts=(), kind=jnp.bfloat16):
    factor_of = shard_levels(own_key, dims, cuts, -0.22, 0.18) if cuts else 1.0
    drawn = jax.random.normal(own_key, dims, jnp.float32) * spread * factor_of
    return jnp.minimum(jnp.maximum(drawn, -bound), bound).astype(kind)


def setup_inputs(seed: int = 0) -> dict:
    splits = jax.random.split(jax.random.key(seed), 7)
    stream = gaussian(splits[0], (TOKENS, CH), 1.0, 6.0, ((0, 64), (1, 4)))
    norm_gain = jnp.clip(1.0 + 0.15 * jax.random.normal(splits[1], (CH,), jnp.float32), 0.25, 1.75)
    short_filters = gaussian(splits[2], (3, KS, CH), KS ** -0.5, 3.5, ((2, 4),), jnp.float32)
    mode_rates = draw_mode_rates(jax.random.fold_in(splits[6], 71), 0)
    residues = draw_residues(jax.random.fold_in(splits[6], 71), 0)
    grad_out = gaussian(splits[5], (TOKENS, CH), 1.0, 6.0, ((0, 64), (1, 4)))
    return {"stream": stream, "norm_gain": norm_gain, "short_filters": short_filters, "mode_rates": mode_rates, "residues": residues, "grad_out": grad_out}


HIGHEST = lax.Precision.HIGHEST
HIGHER = lax.Precision.HIGH
EPSILON = 1e-05

def lag_table(length):
    steps = jnp.arange(length)
    return (steps[:, None, None] - steps[None, :, None] == steps[None, None, :]).astype(jnp.float32)

def filter_tables(decay_rates, residues):
    steps = jnp.arange(P_SIZE).astype(jnp.float32)
    decay_table = jnp.exp(-decay_rates[:, None, :] * steps[None, :, None])
    shifted = jnp.exp(-decay_rates[:, None, :] * (steps[None, :, None] + 1.0))
    response = lax.optimization_barrier(jnp.sum(residues[:, None, :] * decay_table, axis=0))
    toeplitz = jnp.einsum('nc,ijn->ijc', response, lag_table(P_SIZE), precision=HIGHEST)
    step_decay = jnp.exp(-decay_rates * P_SIZE)
    return (decay_table, shifted, toeplitz, step_decay)

def forward_step(toeplitz, carried_table, step_decay, carry_state, inputs):
    one_block, block_end = inputs
    local_part = jnp.einsum('ijc,jc->ic', toeplitz, one_block, precision=HIGHER)
    carried = jnp.einsum('mc,mic->ic', carry_state, carried_table, precision=HIGHEST)
    return (step_decay * carry_state + block_end, (local_part + carried, carry_state))

def backward_step(toeplitz, back_table, step_decay, carry_state, inputs):
    one_block, block_head = inputs
    local_part = jnp.einsum('ijc,ic->jc', toeplitz, one_block, precision=HIGHEST)
    carried = jnp.einsum('mc,mjc->jc', carry_state, back_table, precision=HIGHEST)
    return (step_decay * carry_state + block_head, local_part + carried)

def reference(stream, norm_gain, short_filters, mode_rates, residues, grad_out):
    row_count, chan_count = stream.shape
    block_count = row_count // P_SIZE
    stream_wide = stream.astype(jnp.float32)
    row_scale = lax.rsqrt(lax.optimization_barrier(jnp.sum(stream_wide * stream_wide, axis=1)) / chan_count + EPSILON)
    normed = (stream_wide * row_scale[:, None] * norm_gain[None, :]).astype(jnp.bfloat16)
    padded_half = jnp.concatenate([jnp.zeros((KS - 1, chan_count), jnp.bfloat16), lax.optimization_barrier(normed)], 0)
    padded = padded_half.astype(jnp.float32)
    branches = [sum((short_filters[branch, offset][None, :] * padded[KS - 1 - offset:KS - 1 - offset + row_count] for offset in range(KS))) for branch in range(3)]
    query_part, key_part, value_part = branches
    product = lax.optimization_barrier((key_part * value_part).astype(jnp.bfloat16)).astype(jnp.float32)
    decay_table, shifted, toeplitz, step_decay = filter_tables(mode_rates, residues)
    blocks = product.reshape(block_count, P_SIZE, chan_count)
    block_ends = jnp.einsum('mjc,bjc->bmc', decay_table[:, ::-1, :], blocks, precision=HIGHER)
    zero_state = jnp.zeros((M, chan_count), jnp.float32)
    carried_table = shifted * residues[:, None, :]
    _, (long_conv, starts) = lax.scan(partial(forward_step, toeplitz, carried_table, step_decay), zero_state, (blocks, block_ends))
    long_conv = long_conv.reshape(row_count, chan_count)
    output = (query_part * long_conv).astype(jnp.bfloat16)
    cotangent = grad_out.astype(jnp.float32)
    grad_conv = cotangent * query_part
    grad_query = (cotangent * long_conv).astype(jnp.bfloat16)
    grad_blocks = grad_conv.reshape(block_count, P_SIZE, chan_count)
    block_heads = jnp.einsum('mic,bic->bmc', decay_table, grad_blocks, precision=HIGHEST)
    back_table = carried_table[:, ::-1, :]
    _, grad_product = lax.scan(partial(backward_step, toeplitz, back_table, step_decay), zero_state, (grad_blocks, block_heads), reverse=True)
    grad_product = grad_product.reshape(row_count, chan_count)
    grad_key = (grad_product * value_part).astype(jnp.bfloat16)
    grad_value = (grad_product * key_part).astype(jnp.bfloat16)
    weighted = jnp.einsum('mic,bic->bmc', shifted, grad_blocks, precision=HIGHEST)
    cross_part = lax.optimization_barrier(jnp.sum(weighted * starts, axis=0))
    pairs = jnp.einsum('bic,bjc->ijc', grad_blocks, blocks, precision=HIGHEST)
    by_lag = jnp.einsum('ijc,ijn->nc', pairs, lag_table(P_SIZE), precision=HIGHEST)
    local_part = jnp.einsum('nc,mnc->mc', by_lag, decay_table, precision=HIGHEST)
    norm_factor = 1.0 / jnp.sqrt(jnp.float32(row_count))
    grad_residues = (cross_part + local_part) * norm_factor
    stacked_half = lax.optimization_barrier(jnp.stack([grad_query, grad_key, grad_value], 0))
    stacked = stacked_half.astype(jnp.float32)
    after = jnp.concatenate([stacked, jnp.zeros((3, KS - 1, chan_count), jnp.float32)], 1)
    grad_normed = sum((short_filters[branch, offset][None, :] * after[branch, offset:offset + row_count] for branch in range(3) for offset in range(KS)))
    grad_short = jnp.stack([jnp.einsum('btc,tc->bc', stacked_half, padded_half[KS - 1 - offset:KS - 1 - offset + row_count], preferred_element_type=jnp.float32) for offset in range(KS)], 1) * norm_factor
    row_dot = lax.optimization_barrier(jnp.sum(norm_gain[None, :] * grad_normed * stream_wide, axis=1))
    grad_stream = (row_scale[:, None] * norm_gain[None, :] * grad_normed - stream_wide * (row_scale ** 3 * row_dot / chan_count)[:, None]).astype(jnp.bfloat16)
    return (output, grad_stream, grad_residues, grad_short)
```

```python
import jax
import jax.numpy as jnp
from jax import lax
from jax.sharding import PartitionSpec as P

M = 16
KS = 3
P_SIZE = 32


HIGHEST = lax.Precision.HIGHEST
EPSILON = 1e-05


def passed_along(value, axis, steps):
    count = lax.axis_size(axis)
    first, last = (max(0, -steps), min(count, count - steps))
    return lax.ppermute(value, axis, [(source, source + steps) for source in range(first, last)])


def entering(own, rates, rows, axis, reverse):
    count = lax.axis_size(axis)
    sign = -1 if reverse else 1
    state = passed_along(own, axis, sign)
    shift = 1
    while shift < count:
        decay = jnp.exp(-rates * jnp.float32(rows * shift))
        state = state + decay * passed_along(state, axis, sign * shift)
        shift *= 2
    return state


def summed(value, axis):
    count = lax.axis_size(axis)
    if count & (count - 1):
        return lax.psum(value, axis)
    shift = 1
    while shift < count:
        value = value + lax.ppermute(value, axis, [(i, i ^ shift) for i in range(count)])
        shift *= 2
    return value


def lag_table(length):
    steps = jnp.arange(length)
    return (steps[:, None, None] - steps[None, :, None] == steps[None, None, :]).astype(jnp.float32)


def per_device(stream, norm_gain, short_filters, mode_rates, residues, grad_out):
    row_count, chan_count = stream.shape
    block_count = row_count // P_SIZE
    total_chans = chan_count * lax.axis_size("ch")
    total_rows = row_count * lax.axis_size("ctx")
    stream_wide = stream.astype(jnp.float32)
    squares = lax.psum(jnp.sum(stream_wide * stream_wide, axis=1), "ch")
    row_scale = lax.rsqrt(squares / total_chans + EPSILON)
    normed = (stream_wide * row_scale[:, None] * norm_gain[None, :]).astype(jnp.bfloat16)
    rim_rows = passed_along(normed[row_count - (KS - 1) :], "ctx", 1)
    padded_half = jnp.concatenate([rim_rows, lax.optimization_barrier(normed)], 0)
    padded = padded_half.astype(jnp.float32)
    branches = [
        sum(
            (
                short_filters[branch, offset][None, :]
                * padded[KS - 1 - offset : KS - 1 - offset + row_count]
                for offset in range(KS)
            )
        )
        for branch in range(3)
    ]
    query_part, key_part, value_part = branches
    product = lax.optimization_barrier((key_part * value_part).astype(jnp.bfloat16)).astype(
        jnp.float32
    )
    cotangent = grad_out.astype(jnp.float32)
    grad_conv = cotangent * query_part

    steps = jnp.arange(P_SIZE).astype(jnp.float32)
    decay_table = jnp.exp(-mode_rates[:, None, :] * steps[None, :, None])
    shifted = jnp.exp(-mode_rates[:, None, :] * (steps[None, :, None] + 1.0))
    response = jnp.sum(residues[:, None, :] * decay_table, axis=0)
    lags = steps[:, None] - steps[None, :]
    lag_index = jnp.clip(lags, 0, P_SIZE - 1).astype(jnp.int32)
    toeplitz = jnp.where((lags >= 0)[:, :, None], response[lag_index], 0.0)
    carried_table = shifted * residues[:, None, :]

    blocks = product.reshape(block_count, P_SIZE, chan_count)
    grad_blocks = grad_conv.reshape(block_count, P_SIZE, chan_count)
    block_ends = jnp.sum(decay_table[None, :, ::-1, :] * blocks[:, None], axis=2)
    block_heads = jnp.sum(decay_table[None] * grad_blocks[:, None], axis=2)
    block_steps = jnp.arange(block_count).astype(jnp.float32)
    own_state = jnp.sum(
        jnp.exp(-mode_rates[None] * (P_SIZE * (block_count - 1 - block_steps))[:, None, None])
        * block_ends,
        axis=0,
    )
    own_back = jnp.sum(
        jnp.exp(-mode_rates[None] * (P_SIZE * block_steps)[:, None, None]) * block_heads, axis=0
    )
    incoming = entering(own_state, mode_rates, row_count, "ctx", False)
    later_state = entering(own_back, mode_rates, row_count, "ctx", True)

    gap = block_steps[:, None] - block_steps[None, :] - 1.0
    earlier = (gap >= 0).astype(jnp.float32)
    pair_decay = jnp.exp(
        -mode_rates[None, None] * (P_SIZE * jnp.maximum(gap, 0.0))[:, :, None, None]
    ) * earlier[:, :, None, None]
    starts = jnp.sum(pair_decay * block_ends[None], axis=1) + jnp.exp(
        -mode_rates[None] * (P_SIZE * block_steps)[:, None, None]
    ) * incoming[None]
    later_gap = block_steps[None, :] - block_steps[:, None] - 1.0
    later_mask = (later_gap >= 0).astype(jnp.float32)
    later_decay = jnp.exp(
        -mode_rates[None, None] * (P_SIZE * jnp.maximum(later_gap, 0.0))[:, :, None, None]
    ) * later_mask[:, :, None, None]
    ends_back = jnp.sum(later_decay * block_heads[None], axis=1) + jnp.exp(
        -mode_rates[None] * (P_SIZE * (block_count - 1 - block_steps))[:, None, None]
    ) * later_state[None]

    local_part = jnp.sum(toeplitz[None] * blocks[:, None], axis=2)
    carried = jnp.sum(starts[:, :, None, :] * carried_table[None], axis=1)
    long_conv = (local_part + carried).reshape(row_count, chan_count)
    output = (query_part * long_conv).astype(jnp.bfloat16)
    grad_query = (cotangent * long_conv).astype(jnp.bfloat16)

    back_local = jnp.sum(toeplitz[None] * grad_blocks[:, :, None], axis=1)
    back_carried = jnp.sum(ends_back[:, :, None, :] * carried_table[None, :, ::-1, :], axis=1)
    grad_product = (back_local + back_carried).reshape(row_count, chan_count)
    grad_key = (grad_product * value_part).astype(jnp.bfloat16)
    grad_value = (grad_product * key_part).astype(jnp.bfloat16)

    weighted = jnp.sum(shifted[None] * grad_blocks[:, None], axis=2)
    cross_part = jnp.sum(weighted * starts, axis=0)
    pairs = jnp.einsum("bic,bjc->ijc", grad_blocks, blocks, precision=HIGHEST)
    by_lag = jnp.einsum("ijc,ijn->nc", pairs, lag_table(P_SIZE), precision=HIGHEST)
    local_terms = jnp.sum(by_lag[None] * decay_table, axis=1)

    stacked_half = lax.optimization_barrier(jnp.stack([grad_query, grad_key, grad_value], 0))
    next_rows = passed_along(stacked_half[:, : KS - 1], "ctx", -1)
    stacked = stacked_half.astype(jnp.float32)
    after = jnp.concatenate([stacked, next_rows.astype(jnp.float32)], 1)
    grad_normed = sum(
        (
            short_filters[branch, offset][None, :] * after[branch, offset : offset + row_count]
            for branch in range(3)
            for offset in range(KS)
        )
    )
    short_terms = jnp.stack(
        [
            jnp.einsum(
                "btc,tc->bc",
                stacked_half,
                padded_half[KS - 1 - offset : KS - 1 - offset + row_count],
                preferred_element_type=jnp.float32,
            )
            for offset in range(KS)
        ],
        1,
    )
    partial_sums = jnp.concatenate(
        [cross_part + local_terms, short_terms.reshape(3 * KS, chan_count)], 0
    )
    whole_sums = summed(partial_sums, "ctx")
    norm_factor = 1.0 / jnp.sqrt(jnp.float32(total_rows))
    grad_residues = whole_sums[:M] * norm_factor
    grad_short = whole_sums[M:].reshape(3, KS, chan_count) * norm_factor
    row_dot = lax.psum(jnp.sum(norm_gain[None, :] * grad_normed * stream_wide, axis=1), "ch")
    grad_stream = (
        row_scale[:, None] * norm_gain[None, :] * grad_normed
        - stream_wide * (row_scale**3 * row_dot / total_chans)[:, None]
    ).astype(jnp.bfloat16)
    return (output, grad_stream, grad_residues, grad_short)


def solution(mesh):
    return jax.shard_map(
        per_device,
        mesh=mesh,
        in_specs=(
            P("ctx", "ch"),
            P("ch"),
            P(None, None, "ch"),
            P(None, "ch"),
            P(None, "ch"),
            P("ctx", "ch"),
        ),
        out_specs=(P("ctx", "ch"), P("ctx", "ch"), P(None, "ch"), P(None, None, "ch")),
        check_vma=False,
    )
```

```python
import jax
import jax.numpy as jnp
from jax import lax
from jax.sharding import PartitionSpec as P

M = 16
KS = 3
P_SIZE = 32


HIGHEST = lax.Precision.HIGHEST
EPSILON = 1e-05


def passed_along(value, axis, steps):
    count = lax.axis_size(axis)
    first, last = (max(0, -steps), min(count, count - steps))
    return lax.ppermute(value, axis, [(source, source + steps) for source in range(first, last)])


def radices(count):
    levels = []
    while count > 1:
        radix = 4 if count % 4 == 0 else 2
        levels.append(radix)
        count //= radix
    return levels


def members(value, axis, stride, radix):
    count = lax.axis_size(axis)
    digit = (lax.axis_index(axis) // stride) % radix
    received = [value]
    for step in range(1, radix):
        pairs = []
        for source in range(count):
            source_digit = (source // stride) % radix
            target = source + (((source_digit - step) % radix) - source_digit) * stride
            pairs.append((source, target))
        received.append(lax.ppermute(value, axis, pairs))
    ordered = [
        lax.select_n(((position - digit) % radix).astype(jnp.int32), *received)
        for position in range(radix)
    ]
    return ordered, digit


def power_of_two(count):
    return count & (count - 1) == 0


def entering(own_state, own_back, rates, rows, axis):
    count = lax.axis_size(axis)
    place = lax.axis_index(axis)
    incoming = jnp.zeros_like(own_state)
    later = jnp.zeros_like(own_back)
    totals = jnp.stack([own_state, own_back], 0)
    stride = 1
    for radix in radices(count):
        group, digit = members(totals, axis, stride, radix)
        position = (place % stride).astype(jnp.float32)
        for other in range(radix):
            before = (digit > other).astype(jnp.float32)
            after = (digit < other).astype(jnp.float32)
            ahead = jnp.maximum(digit - 1 - other, 0).astype(jnp.float32) * stride + position
            behind = jnp.maximum(other - 1 - digit, 0).astype(jnp.float32) * stride + (
                stride - 1 - position
            )
            incoming = incoming + before * jnp.exp(-rates * (rows * ahead)) * group[other][0]
            later = later + after * jnp.exp(-rates * (rows * behind)) * group[other][1]
        forward_total = group[0][0]
        backward_total = group[0][1]
        for other in range(1, radix):
            forward_total = (
                jnp.exp(-rates * jnp.float32(rows * stride)) * forward_total + group[other][0]
            )
            backward_total = backward_total + jnp.exp(
                -rates * jnp.float32(rows * stride * other)
            ) * group[other][1]
        totals = jnp.stack([forward_total, backward_total], 0)
        stride *= radix
    return incoming, later


def summed(value, axis):
    count = lax.axis_size(axis)
    if not power_of_two(count):
        return lax.psum(value, axis)
    stride = 1
    for radix in radices(count):
        group, _ = members(value, axis, stride, radix)
        if radix == 4:
            value = (group[0] + group[1]) + (group[2] + group[3])
        else:
            value = group[0] + group[1]
        stride *= radix
    return value


def lag_table(length):
    steps = jnp.arange(length)
    return (steps[:, None, None] - steps[None, :, None] == steps[None, None, :]).astype(jnp.float32)


def per_device(stream, norm_gain, short_filters, mode_rates, residues, grad_out):
    row_count, chan_count = stream.shape
    block_count = row_count // P_SIZE
    total_chans = chan_count * lax.axis_size("ch")
    total_rows = row_count * lax.axis_size("ctx")
    stream_wide = stream.astype(jnp.float32)
    squares = summed(jnp.sum(stream_wide * stream_wide, axis=1), "ch")
    row_scale = lax.rsqrt(squares / total_chans + EPSILON)
    normed = (stream_wide * row_scale[:, None] * norm_gain[None, :]).astype(jnp.bfloat16)
    rim_rows = passed_along(normed[row_count - (KS - 1) :], "ctx", 1)
    padded_half = jnp.concatenate([rim_rows, lax.optimization_barrier(normed)], 0)
    padded = padded_half.astype(jnp.float32)
    branches = [
        sum(
            (
                short_filters[branch, offset][None, :]
                * padded[KS - 1 - offset : KS - 1 - offset + row_count]
                for offset in range(KS)
            )
        )
        for branch in range(3)
    ]
    query_part, key_part, value_part = branches
    product = lax.optimization_barrier((key_part * value_part).astype(jnp.bfloat16)).astype(
        jnp.float32
    )
    cotangent = grad_out.astype(jnp.float32)
    grad_conv = cotangent * query_part

    steps = jnp.arange(P_SIZE).astype(jnp.float32)
    decay_table = jnp.exp(-mode_rates[:, None, :] * steps[None, :, None])
    shifted = jnp.exp(-mode_rates[:, None, :] * (steps[None, :, None] + 1.0))
    response = jnp.sum(residues[:, None, :] * decay_table, axis=0)
    lags = steps[:, None] - steps[None, :]
    lag_index = jnp.clip(lags, 0, P_SIZE - 1).astype(jnp.int32)
    toeplitz = jnp.where((lags >= 0)[:, :, None], response[lag_index], 0.0)
    carried_table = shifted * residues[:, None, :]

    blocks = product.reshape(block_count, P_SIZE, chan_count)
    grad_blocks = grad_conv.reshape(block_count, P_SIZE, chan_count)
    block_ends = jnp.sum(decay_table[None, :, ::-1, :] * blocks[:, None], axis=2)
    block_heads = jnp.sum(decay_table[None] * grad_blocks[:, None], axis=2)
    block_steps = jnp.arange(block_count).astype(jnp.float32)
    own_state = jnp.sum(
        jnp.exp(-mode_rates[None] * (P_SIZE * (block_count - 1 - block_steps))[:, None, None])
        * block_ends,
        axis=0,
    )
    own_back = jnp.sum(
        jnp.exp(-mode_rates[None] * (P_SIZE * block_steps)[:, None, None]) * block_heads, axis=0
    )
    incoming, later_state = entering(own_state, own_back, mode_rates, row_count, "ctx")

    gap = block_steps[:, None] - block_steps[None, :] - 1.0
    earlier = (gap >= 0).astype(jnp.float32)
    pair_decay = jnp.exp(
        -mode_rates[None, None] * (P_SIZE * jnp.maximum(gap, 0.0))[:, :, None, None]
    ) * earlier[:, :, None, None]
    starts = jnp.sum(pair_decay * block_ends[None], axis=1) + jnp.exp(
        -mode_rates[None] * (P_SIZE * block_steps)[:, None, None]
    ) * incoming[None]
    later_gap = block_steps[None, :] - block_steps[:, None] - 1.0
    later_mask = (later_gap >= 0).astype(jnp.float32)
    later_decay = jnp.exp(
        -mode_rates[None, None] * (P_SIZE * jnp.maximum(later_gap, 0.0))[:, :, None, None]
    ) * later_mask[:, :, None, None]
    ends_back = jnp.sum(later_decay * block_heads[None], axis=1) + jnp.exp(
        -mode_rates[None] * (P_SIZE * (block_count - 1 - block_steps))[:, None, None]
    ) * later_state[None]

    local_part = jnp.sum(toeplitz[None] * blocks[:, None], axis=2)
    carried = jnp.sum(starts[:, :, None, :] * carried_table[None], axis=1)
    long_conv = (local_part + carried).reshape(row_count, chan_count)
    output = (query_part * long_conv).astype(jnp.bfloat16)
    grad_query = (cotangent * long_conv).astype(jnp.bfloat16)

    back_local = jnp.sum(toeplitz[None] * grad_blocks[:, :, None], axis=1)
    back_carried = jnp.sum(ends_back[:, :, None, :] * carried_table[None, :, ::-1, :], axis=1)
    grad_product = (back_local + back_carried).reshape(row_count, chan_count)
    grad_key = (grad_product * value_part).astype(jnp.bfloat16)
    grad_value = (grad_product * key_part).astype(jnp.bfloat16)

    weighted = jnp.sum(shifted[None] * grad_blocks[:, None], axis=2)
    cross_part = jnp.sum(weighted * starts, axis=0)
    pairs = jnp.einsum("bic,bjc->ijc", grad_blocks, blocks, precision=HIGHEST)
    by_lag = jnp.einsum("ijc,ijn->nc", pairs, lag_table(P_SIZE), precision=HIGHEST)
    local_terms = jnp.sum(by_lag[None] * decay_table, axis=1)

    stacked_half = lax.optimization_barrier(jnp.stack([grad_query, grad_key, grad_value], 0))
    next_rows = passed_along(stacked_half[:, : KS - 1], "ctx", -1)
    stacked = stacked_half.astype(jnp.float32)
    after = jnp.concatenate([stacked, next_rows.astype(jnp.float32)], 1)
    grad_normed = sum(
        (
            short_filters[branch, offset][None, :] * after[branch, offset : offset + row_count]
            for branch in range(3)
            for offset in range(KS)
        )
    )
    short_terms = jnp.stack(
        [
            jnp.einsum(
                "btc,tc->bc",
                stacked_half,
                padded_half[KS - 1 - offset : KS - 1 - offset + row_count],
                preferred_element_type=jnp.float32,
            )
            for offset in range(KS)
        ],
        1,
    )
    partial_sums = jnp.concatenate(
        [cross_part + local_terms, short_terms.reshape(3 * KS, chan_count)], 0
    )
    whole_sums = summed(partial_sums, "ctx")
    norm_factor = 1.0 / jnp.sqrt(jnp.float32(total_rows))
    grad_residues = whole_sums[:M] * norm_factor
    grad_short = whole_sums[M:].reshape(3, KS, chan_count) * norm_factor
    row_dot = summed(jnp.sum(norm_gain[None, :] * grad_normed * stream_wide, axis=1), "ch")
    grad_stream = (
        row_scale[:, None] * norm_gain[None, :] * grad_normed
        - stream_wide * (row_scale**3 * row_dot / total_chans)[:, None]
    ).astype(jnp.bfloat16)
    return (output, grad_stream, grad_residues, grad_short)


def solution(mesh):
    return jax.shard_map(
        per_device,
        mesh=mesh,
        in_specs=(
            P("ctx", "ch"),
            P("ch"),
            P(None, None, "ch"),
            P(None, "ch"),
            P(None, "ch"),
            P("ctx", "ch"),
        ),
        out_specs=(P("ctx", "ch"), P("ctx", "ch"), P(None, "ch"), P(None, None, "ch")),
        check_vma=False,
    )
```

```python
import jax
import jax.numpy as jnp
from jax import lax
from jax.sharding import PartitionSpec as P

M = 16
KS = 3
P_SIZE = 32


EPSILON = 1e-05


def passed_along(value, axis, steps):
    count = lax.axis_size(axis)
    first, last = (max(0, -steps), min(count, count - steps))
    return lax.ppermute(value, axis, [(source, source + steps) for source in range(first, last)])


def radices(count):
    levels = []
    while count > 1:
        radix = 4 if count % 4 == 0 else 2
        levels.append(radix)
        count //= radix
    return levels


def members(value, axis, stride, radix):
    count = lax.axis_size(axis)
    digit = (lax.axis_index(axis) // stride) % radix
    received = [value]
    for step in range(1, radix):
        pairs = []
        for source in range(count):
            source_digit = (source // stride) % radix
            target = source + (((source_digit - step) % radix) - source_digit) * stride
            pairs.append((source, target))
        received.append(lax.ppermute(value, axis, pairs))
    ordered = [
        lax.select_n(((position - digit) % radix).astype(jnp.int32), *received)
        for position in range(radix)
    ]
    return ordered, digit


def power_of_two(count):
    return count & (count - 1) == 0


def entering(own_state, own_back, rates, rows, axis):
    count = lax.axis_size(axis)
    place = lax.axis_index(axis)
    incoming = jnp.zeros_like(own_state)
    later = jnp.zeros_like(own_back)
    totals = jnp.stack([own_state, own_back], 0)
    stride = 1
    for radix in radices(count):
        group, digit = members(totals, axis, stride, radix)
        position = (place % stride).astype(jnp.float32)
        for other in range(radix):
            before = (digit > other).astype(jnp.float32)
            after = (digit < other).astype(jnp.float32)
            ahead = jnp.maximum(digit - 1 - other, 0).astype(jnp.float32) * stride + position
            behind = jnp.maximum(other - 1 - digit, 0).astype(jnp.float32) * stride + (
                stride - 1 - position
            )
            incoming = incoming + before * jnp.exp(-rates * (rows * ahead)) * group[other][0]
            later = later + after * jnp.exp(-rates * (rows * behind)) * group[other][1]
        forward_total = group[0][0]
        backward_total = group[0][1]
        for other in range(1, radix):
            forward_total = (
                jnp.exp(-rates * jnp.float32(rows * stride)) * forward_total + group[other][0]
            )
            backward_total = backward_total + jnp.exp(
                -rates * jnp.float32(rows * stride * other)
            ) * group[other][1]
        totals = jnp.stack([forward_total, backward_total], 0)
        stride *= radix
    return incoming, later


def summed(value, axis):
    count = lax.axis_size(axis)
    if not power_of_two(count):
        return lax.psum(value, axis)
    stride = 1
    for radix in radices(count):
        group, _ = members(value, axis, stride, radix)
        if radix == 4:
            value = (group[0] + group[1]) + (group[2] + group[3])
        else:
            value = group[0] + group[1]
        stride *= radix
    return value


def per_device(stream, norm_gain, short_filters, mode_rates, residues, grad_out):
    row_count, chan_count = stream.shape
    block_count = row_count // P_SIZE
    total_chans = chan_count * lax.axis_size("ch")
    total_rows = row_count * lax.axis_size("ctx")
    stream_wide = stream.astype(jnp.float32)
    squares = summed(jnp.sum(stream_wide * stream_wide, axis=1), "ch")
    row_scale = lax.rsqrt(squares / total_chans + EPSILON)
    normed = (stream_wide * row_scale[:, None] * norm_gain[None, :]).astype(jnp.bfloat16)
    rim_rows = passed_along(normed[row_count - (KS - 1) :], "ctx", 1)
    padded_half = jnp.concatenate([rim_rows, lax.optimization_barrier(normed)], 0)
    padded = padded_half.astype(jnp.float32)
    branches = [
        sum(
            (
                short_filters[branch, offset][None, :]
                * padded[KS - 1 - offset : KS - 1 - offset + row_count]
                for offset in range(KS)
            )
        )
        for branch in range(3)
    ]
    query_part, key_part, value_part = branches
    product = lax.optimization_barrier((key_part * value_part).astype(jnp.bfloat16)).astype(
        jnp.float32
    )
    cotangent = grad_out.astype(jnp.float32)
    grad_conv = cotangent * query_part

    steps = jnp.arange(P_SIZE).astype(jnp.float32)
    decay_table = jnp.exp(-mode_rates[:, None, :] * steps[None, :, None])
    decay_reversed = jnp.exp(-mode_rates[:, None, :] * (P_SIZE - 1.0 - steps)[None, :, None])
    shifted = jnp.exp(-mode_rates[:, None, :] * (steps[None, :, None] + 1.0))
    response = jnp.sum(residues[:, None, :] * decay_table, axis=0)
    carried_table = shifted * residues[:, None, :]
    carried_reversed = (
        jnp.exp(-mode_rates[:, None, :] * (P_SIZE - steps)[None, :, None]) * residues[:, None, :]
    )

    blocks = product.reshape(block_count, P_SIZE, chan_count)
    grad_blocks = grad_conv.reshape(block_count, P_SIZE, chan_count)
    block_ends = jnp.sum(decay_reversed[None] * blocks[:, None], axis=2)
    block_heads = jnp.sum(decay_table[None] * grad_blocks[:, None], axis=2)
    block_steps = jnp.arange(block_count).astype(jnp.float32)
    own_state = jnp.sum(
        jnp.exp(-mode_rates[None] * (P_SIZE * (block_count - 1 - block_steps))[:, None, None])
        * block_ends,
        axis=0,
    )
    own_back = jnp.sum(
        jnp.exp(-mode_rates[None] * (P_SIZE * block_steps)[:, None, None]) * block_heads, axis=0
    )
    incoming, later_state = entering(own_state, own_back, mode_rates, row_count, "ctx")

    gap = block_steps[:, None] - block_steps[None, :] - 1.0
    earlier = (gap >= 0).astype(jnp.float32)
    pair_decay = jnp.exp(
        -mode_rates[None, None] * (P_SIZE * jnp.maximum(gap, 0.0))[:, :, None, None]
    ) * earlier[:, :, None, None]
    starts = jnp.sum(pair_decay * block_ends[None], axis=1) + jnp.exp(
        -mode_rates[None] * (P_SIZE * block_steps)[:, None, None]
    ) * incoming[None]
    later_gap = block_steps[None, :] - block_steps[:, None] - 1.0
    later_mask = (later_gap >= 0).astype(jnp.float32)
    later_decay = jnp.exp(
        -mode_rates[None, None] * (P_SIZE * jnp.maximum(later_gap, 0.0))[:, :, None, None]
    ) * later_mask[:, :, None, None]
    ends_back = jnp.sum(later_decay * block_heads[None], axis=1) + jnp.exp(
        -mode_rates[None] * (P_SIZE * (block_count - 1 - block_steps))[:, None, None]
    ) * later_state[None]

    lead = jnp.zeros((block_count, P_SIZE - 1, chan_count), jnp.float32)
    blocks_padded = jnp.concatenate([lead, blocks], 1)
    grads_padded = jnp.concatenate([grad_blocks, lead], 1)
    local_part = sum(
        response[lag][None, None, :] * blocks_padded[:, P_SIZE - 1 - lag : 2 * P_SIZE - 1 - lag]
        for lag in range(P_SIZE)
    )
    carried = jnp.sum(starts[:, :, None, :] * carried_table[None], axis=1)
    long_conv = (local_part + carried).reshape(row_count, chan_count)
    output = (query_part * long_conv).astype(jnp.bfloat16)
    grad_query = (cotangent * long_conv).astype(jnp.bfloat16)

    back_local = sum(
        response[lag][None, None, :] * grads_padded[:, lag : lag + P_SIZE] for lag in range(P_SIZE)
    )
    back_carried = jnp.sum(ends_back[:, :, None, :] * carried_reversed[None], axis=1)
    grad_product = (back_local + back_carried).reshape(row_count, chan_count)
    grad_key = (grad_product * value_part).astype(jnp.bfloat16)
    grad_value = (grad_product * key_part).astype(jnp.bfloat16)

    weighted = jnp.sum(shifted[None] * grad_blocks[:, None], axis=2)
    cross_part = jnp.sum(weighted * starts, axis=0)
    by_lag = jnp.stack(
        [
            jnp.sum(
                blocks_padded[:, P_SIZE - 1 - lag : 2 * P_SIZE - 1 - lag] * grad_blocks, axis=(0, 1)
            )
            for lag in range(P_SIZE)
        ],
        0,
    )
    local_terms = jnp.sum(by_lag[None] * decay_table, axis=1)

    stacked_half = lax.optimization_barrier(jnp.stack([grad_query, grad_key, grad_value], 0))
    next_rows = passed_along(stacked_half[:, : KS - 1], "ctx", -1)
    stacked = stacked_half.astype(jnp.float32)
    after = jnp.concatenate([stacked, next_rows.astype(jnp.float32)], 1)
    grad_normed = sum(
        (
            short_filters[branch, offset][None, :] * after[branch, offset : offset + row_count]
            for branch in range(3)
            for offset in range(KS)
        )
    )
    short_terms = jnp.stack(
        [
            jnp.einsum(
                "btc,tc->bc",
                stacked_half,
                padded_half[KS - 1 - offset : KS - 1 - offset + row_count],
                preferred_element_type=jnp.float32,
            )
            for offset in range(KS)
        ],
        1,
    )
    partial_sums = jnp.concatenate(
        [cross_part + local_terms, short_terms.reshape(3 * KS, chan_count)], 0
    )
    whole_sums = summed(partial_sums, "ctx")
    norm_factor = 1.0 / jnp.sqrt(jnp.float32(total_rows))
    grad_residues = whole_sums[:M] * norm_factor
    grad_short = whole_sums[M:].reshape(3, KS, chan_count) * norm_factor
    row_dot = summed(jnp.sum(norm_gain[None, :] * grad_normed * stream_wide, axis=1), "ch")
    grad_stream = (
        row_scale[:, None] * norm_gain[None, :] * grad_normed
        - stream_wide * (row_scale**3 * row_dot / total_chans)[:, None]
    ).astype(jnp.bfloat16)
    return (output, grad_stream, grad_residues, grad_short)


def solution(mesh):
    return jax.shard_map(
        per_device,
        mesh=mesh,
        in_specs=(
            P("ctx", "ch"),
            P("ch"),
            P(None, None, "ch"),
            P(None, "ch"),
            P(None, "ch"),
            P("ctx", "ch"),
        ),
        out_specs=(P("ctx", "ch"), P("ctx", "ch"), P(None, "ch"), P(None, None, "ch")),
        check_vma=False,
    )
```

```python
import jax
import jax.numpy as jnp
from jax import lax
from jax.sharding import PartitionSpec as P

M = 16
KS = 3
P_SIZE = 32


EPSILON = 1e-05


def passed_along(value, axis, steps):
    count = lax.axis_size(axis)
    first, last = (max(0, -steps), min(count, count - steps))
    return lax.ppermute(value, axis, [(source, source + steps) for source in range(first, last)])


def radices(count):
    levels = []
    while count > 1:
        radix = 4 if count % 4 == 0 else 2
        levels.append(radix)
        count //= radix
    return levels


def members(value, axis, stride, radix):
    count = lax.axis_size(axis)
    digit = (lax.axis_index(axis) // stride) % radix
    received = [value]
    for step in range(1, radix):
        pairs = []
        for source in range(count):
            source_digit = (source // stride) % radix
            target = source + (((source_digit - step) % radix) - source_digit) * stride
            pairs.append((source, target))
        received.append(lax.ppermute(value, axis, pairs))
    ordered = [
        lax.select_n(((position - digit) % radix).astype(jnp.int32), *received)
        for position in range(radix)
    ]
    return ordered, digit


def power_of_two(count):
    return count & (count - 1) == 0


def entering(own_state, own_back, rates, rows, axis):
    count = lax.axis_size(axis)
    place = lax.axis_index(axis)
    incoming = jnp.zeros_like(own_state)
    later = jnp.zeros_like(own_back)
    totals = jnp.stack([own_state, own_back], 0)
    stride = 1
    for radix in radices(count):
        group, digit = members(totals, axis, stride, radix)
        position = (place % stride).astype(jnp.float32)
        for other in range(radix):
            before = (digit > other).astype(jnp.float32)
            after = (digit < other).astype(jnp.float32)
            ahead = jnp.maximum(digit - 1 - other, 0).astype(jnp.float32) * stride + position
            behind = jnp.maximum(other - 1 - digit, 0).astype(jnp.float32) * stride + (
                stride - 1 - position
            )
            incoming = incoming + before * jnp.exp(-rates * (rows * ahead)) * group[other][0]
            later = later + after * jnp.exp(-rates * (rows * behind)) * group[other][1]
        forward_total = group[0][0]
        backward_total = group[0][1]
        for other in range(1, radix):
            forward_total = (
                jnp.exp(-rates * jnp.float32(rows * stride)) * forward_total + group[other][0]
            )
            backward_total = backward_total + jnp.exp(
                -rates * jnp.float32(rows * stride * other)
            ) * group[other][1]
        totals = jnp.stack([forward_total, backward_total], 0)
        stride *= radix
    return incoming, later


def summed(value, axis):
    count = lax.axis_size(axis)
    flat = value.reshape(-1)
    width = -(-flat.size // count)
    width = -(-width // 128) * 128
    flat = jnp.pad(flat, (0, count * width - flat.size)).reshape(count, width)
    pieces = lax.all_to_all(flat, axis, 0, 0)
    own = jnp.sum(pieces, axis=0)
    whole = lax.all_to_all(jnp.broadcast_to(own[None], (count, width)), axis, 0, 0)
    return whole.reshape(-1)[: value.size].reshape(value.shape)


def per_device(stream, norm_gain, short_filters, mode_rates, residues, grad_out):
    row_count, chan_count = stream.shape
    block_count = row_count // P_SIZE
    total_chans = chan_count * lax.axis_size("ch")
    total_rows = row_count * lax.axis_size("ctx")
    stream_wide = stream.astype(jnp.float32)
    squares = summed(jnp.sum(stream_wide * stream_wide, axis=1), "ch")
    row_scale = lax.rsqrt(squares / total_chans + EPSILON)
    normed = (stream_wide * row_scale[:, None] * norm_gain[None, :]).astype(jnp.bfloat16)
    rim_rows = passed_along(normed[row_count - (KS - 1) :], "ctx", 1)
    padded_half = jnp.concatenate([rim_rows, lax.optimization_barrier(normed)], 0)
    padded = padded_half.astype(jnp.float32)
    branches = [
        sum(
            (
                short_filters[branch, offset][None, :]
                * padded[KS - 1 - offset : KS - 1 - offset + row_count]
                for offset in range(KS)
            )
        )
        for branch in range(3)
    ]
    query_part, key_part, value_part = branches
    product = lax.optimization_barrier((key_part * value_part).astype(jnp.bfloat16)).astype(
        jnp.float32
    )
    cotangent = grad_out.astype(jnp.float32)
    grad_conv = cotangent * query_part

    steps = jnp.arange(P_SIZE).astype(jnp.float32)
    decay_table = jnp.exp(-mode_rates[:, None, :] * steps[None, :, None])
    decay_reversed = jnp.exp(-mode_rates[:, None, :] * (P_SIZE - 1.0 - steps)[None, :, None])
    shifted = jnp.exp(-mode_rates[:, None, :] * (steps[None, :, None] + 1.0))
    response = jnp.sum(residues[:, None, :] * decay_table, axis=0)
    carried_table = shifted * residues[:, None, :]
    carried_reversed = (
        jnp.exp(-mode_rates[:, None, :] * (P_SIZE - steps)[None, :, None]) * residues[:, None, :]
    )

    blocks = product.reshape(block_count, P_SIZE, chan_count)
    grad_blocks = grad_conv.reshape(block_count, P_SIZE, chan_count)
    block_ends = jnp.sum(decay_reversed[None] * blocks[:, None], axis=2)
    block_heads = jnp.sum(decay_table[None] * grad_blocks[:, None], axis=2)
    block_steps = jnp.arange(block_count).astype(jnp.float32)
    own_state = jnp.sum(
        jnp.exp(-mode_rates[None] * (P_SIZE * (block_count - 1 - block_steps))[:, None, None])
        * block_ends,
        axis=0,
    )
    own_back = jnp.sum(
        jnp.exp(-mode_rates[None] * (P_SIZE * block_steps)[:, None, None]) * block_heads, axis=0
    )
    incoming, later_state = entering(own_state, own_back, mode_rates, row_count, "ctx")

    gap = block_steps[:, None] - block_steps[None, :] - 1.0
    earlier = (gap >= 0).astype(jnp.float32)
    pair_decay = jnp.exp(
        -mode_rates[None, None] * (P_SIZE * jnp.maximum(gap, 0.0))[:, :, None, None]
    ) * earlier[:, :, None, None]
    starts = jnp.sum(pair_decay * block_ends[None], axis=1) + jnp.exp(
        -mode_rates[None] * (P_SIZE * block_steps)[:, None, None]
    ) * incoming[None]
    later_gap = block_steps[None, :] - block_steps[:, None] - 1.0
    later_mask = (later_gap >= 0).astype(jnp.float32)
    later_decay = jnp.exp(
        -mode_rates[None, None] * (P_SIZE * jnp.maximum(later_gap, 0.0))[:, :, None, None]
    ) * later_mask[:, :, None, None]
    ends_back = jnp.sum(later_decay * block_heads[None], axis=1) + jnp.exp(
        -mode_rates[None] * (P_SIZE * (block_count - 1 - block_steps))[:, None, None]
    ) * later_state[None]

    lead = jnp.zeros((block_count, P_SIZE - 1, chan_count), jnp.float32)
    blocks_padded = jnp.concatenate([lead, blocks], 1)
    grads_padded = jnp.concatenate([grad_blocks, lead], 1)
    local_part = sum(
        response[lag][None, None, :] * blocks_padded[:, P_SIZE - 1 - lag : 2 * P_SIZE - 1 - lag]
        for lag in range(P_SIZE)
    )
    carried = jnp.sum(starts[:, :, None, :] * carried_table[None], axis=1)
    long_conv = (local_part + carried).reshape(row_count, chan_count)
    output = (query_part * long_conv).astype(jnp.bfloat16)
    grad_query = (cotangent * long_conv).astype(jnp.bfloat16)

    back_local = sum(
        response[lag][None, None, :] * grads_padded[:, lag : lag + P_SIZE] for lag in range(P_SIZE)
    )
    back_carried = jnp.sum(ends_back[:, :, None, :] * carried_reversed[None], axis=1)
    grad_product = (back_local + back_carried).reshape(row_count, chan_count)
    grad_key = (grad_product * value_part).astype(jnp.bfloat16)
    grad_value = (grad_product * key_part).astype(jnp.bfloat16)

    weighted = jnp.sum(shifted[None] * grad_blocks[:, None], axis=2)
    cross_part = jnp.sum(weighted * starts, axis=0)
    by_lag = jnp.stack(
        [
            jnp.sum(
                blocks_padded[:, P_SIZE - 1 - lag : 2 * P_SIZE - 1 - lag] * grad_blocks, axis=(0, 1)
            )
            for lag in range(P_SIZE)
        ],
        0,
    )
    local_terms = jnp.sum(by_lag[None] * decay_table, axis=1)

    stacked_half = lax.optimization_barrier(jnp.stack([grad_query, grad_key, grad_value], 0))
    next_rows = passed_along(stacked_half[:, : KS - 1], "ctx", -1)
    stacked = stacked_half.astype(jnp.float32)
    after = jnp.concatenate([stacked, next_rows.astype(jnp.float32)], 1)
    grad_normed = sum(
        (
            short_filters[branch, offset][None, :] * after[branch, offset : offset + row_count]
            for branch in range(3)
            for offset in range(KS)
        )
    )
    short_terms = jnp.stack(
        [
            jnp.einsum(
                "btc,tc->bc",
                stacked_half,
                padded_half[KS - 1 - offset : KS - 1 - offset + row_count],
                preferred_element_type=jnp.float32,
            )
            for offset in range(KS)
        ],
        1,
    )
    partial_sums = jnp.concatenate(
        [cross_part + local_terms, short_terms.reshape(3 * KS, chan_count)], 0
    )
    whole_sums = summed(partial_sums, "ctx")
    norm_factor = 1.0 / jnp.sqrt(jnp.float32(total_rows))
    grad_residues = whole_sums[:M] * norm_factor
    grad_short = whole_sums[M:].reshape(3, KS, chan_count) * norm_factor
    row_dot = summed(jnp.sum(norm_gain[None, :] * grad_normed * stream_wide, axis=1), "ch")
    grad_stream = (
        row_scale[:, None] * norm_gain[None, :] * grad_normed
        - stream_wide * (row_scale**3 * row_dot / total_chans)[:, None]
    ).astype(jnp.bfloat16)
    return (output, grad_stream, grad_residues, grad_short)


def solution(mesh):
    return jax.shard_map(
        per_device,
        mesh=mesh,
        in_specs=(
            P("ctx", "ch"),
            P("ch"),
            P(None, None, "ch"),
            P(None, "ch"),
            P(None, "ch"),
            P("ctx", "ch"),
        ),
        out_specs=(P("ctx", "ch"), P("ctx", "ch"), P(None, "ch"), P(None, None, "ch")),
        check_vma=False,
    )
```

```python
import jax
import jax.numpy as jnp
from jax import lax
from jax.sharding import PartitionSpec as P

M = 16
KS = 3
P_SIZE = 32


EPSILON = 1e-05


def passed_along(value, axis, steps):
    count = lax.axis_size(axis)
    first, last = (max(0, -steps), min(count, count - steps))
    return lax.ppermute(value, axis, [(source, source + steps) for source in range(first, last)])


def radices(count):
    levels = []
    while count > 1:
        radix = 4 if count % 4 == 0 else 2
        levels.append(radix)
        count //= radix
    return levels


def members(value, axis, stride, radix):
    count = lax.axis_size(axis)
    digit = (lax.axis_index(axis) // stride) % radix
    received = [value]
    for step in range(1, radix):
        pairs = []
        for source in range(count):
            source_digit = (source // stride) % radix
            target = source + (((source_digit - step) % radix) - source_digit) * stride
            pairs.append((source, target))
        received.append(lax.ppermute(value, axis, pairs))
    ordered = [
        lax.select_n(((position - digit) % radix).astype(jnp.int32), *received)
        for position in range(radix)
    ]
    return ordered, digit


def power_of_two(count):
    return count & (count - 1) == 0


def entering(own_state, own_back, rates, rows, axis):
    count = lax.axis_size(axis)
    place = lax.axis_index(axis)
    incoming = jnp.zeros_like(own_state)
    later = jnp.zeros_like(own_back)
    totals = jnp.stack([own_state, own_back], 0)
    stride = 1
    for radix in radices(count):
        group, digit = members(totals, axis, stride, radix)
        position = (place % stride).astype(jnp.float32)
        for other in range(radix):
            before = (digit > other).astype(jnp.float32)
            after = (digit < other).astype(jnp.float32)
            ahead = jnp.maximum(digit - 1 - other, 0).astype(jnp.float32) * stride + position
            behind = jnp.maximum(other - 1 - digit, 0).astype(jnp.float32) * stride + (
                stride - 1 - position
            )
            incoming = incoming + before * jnp.exp(-rates * (rows * ahead)) * group[other][0]
            later = later + after * jnp.exp(-rates * (rows * behind)) * group[other][1]
        forward_total = group[0][0]
        backward_total = group[0][1]
        for other in range(1, radix):
            forward_total = (
                jnp.exp(-rates * jnp.float32(rows * stride)) * forward_total + group[other][0]
            )
            backward_total = backward_total + jnp.exp(
                -rates * jnp.float32(rows * stride * other)
            ) * group[other][1]
        totals = jnp.stack([forward_total, backward_total], 0)
        stride *= radix
    return incoming, later


def summed(value, axis):
    count = lax.axis_size(axis)
    if not power_of_two(count):
        return lax.psum(value, axis)
    stride = 1
    for radix in radices(count):
        group, _ = members(value, axis, stride, radix)
        if radix == 4:
            value = (group[0] + group[1]) + (group[2] + group[3])
        else:
            value = group[0] + group[1]
        stride *= radix
    return value


def per_device(stream, norm_gain, short_filters, mode_rates, residues, grad_out):
    row_count, chan_count = stream.shape
    block_count = row_count // P_SIZE
    total_chans = chan_count * lax.axis_size("ch")
    total_rows = row_count * lax.axis_size("ctx")
    stream_wide = stream.astype(jnp.float32)
    rim_rows = passed_along(stream[row_count - (KS - 1) :], "ctx", 1)
    with_rim = jnp.concatenate([rim_rows, stream], 0).astype(jnp.float32)
    squares = summed(jnp.sum(with_rim * with_rim, axis=1), "ch")
    scale_with_rim = lax.rsqrt(squares / total_chans + EPSILON)
    row_scale = scale_with_rim[KS - 1 :]
    padded_half = lax.optimization_barrier(
        (with_rim * scale_with_rim[:, None] * norm_gain[None, :]).astype(jnp.bfloat16)
    )
    padded = padded_half.astype(jnp.float32)
    branches = [
        sum(
            (
                short_filters[branch, offset][None, :]
                * padded[KS - 1 - offset : KS - 1 - offset + row_count]
                for offset in range(KS)
            )
        )
        for branch in range(3)
    ]
    query_part, key_part, value_part = branches
    product = lax.optimization_barrier((key_part * value_part).astype(jnp.bfloat16)).astype(
        jnp.float32
    )
    cotangent = grad_out.astype(jnp.float32)
    grad_conv = cotangent * query_part

    steps = jnp.arange(P_SIZE).astype(jnp.float32)
    decay_table = jnp.exp(-mode_rates[:, None, :] * steps[None, :, None])
    decay_reversed = jnp.exp(-mode_rates[:, None, :] * (P_SIZE - 1.0 - steps)[None, :, None])
    shifted = jnp.exp(-mode_rates[:, None, :] * (steps[None, :, None] + 1.0))
    response = jnp.sum(residues[:, None, :] * decay_table, axis=0)
    carried_table = shifted * residues[:, None, :]
    carried_reversed = (
        jnp.exp(-mode_rates[:, None, :] * (P_SIZE - steps)[None, :, None]) * residues[:, None, :]
    )

    blocks = product.reshape(block_count, P_SIZE, chan_count)
    grad_blocks = grad_conv.reshape(block_count, P_SIZE, chan_count)
    block_ends = jnp.sum(decay_reversed[None] * blocks[:, None], axis=2)
    block_heads = jnp.sum(decay_table[None] * grad_blocks[:, None], axis=2)
    block_steps = jnp.arange(block_count).astype(jnp.float32)
    own_state = jnp.sum(
        jnp.exp(-mode_rates[None] * (P_SIZE * (block_count - 1 - block_steps))[:, None, None])
        * block_ends,
        axis=0,
    )
    own_back = jnp.sum(
        jnp.exp(-mode_rates[None] * (P_SIZE * block_steps)[:, None, None]) * block_heads, axis=0
    )
    incoming, later_state = entering(own_state, own_back, mode_rates, row_count, "ctx")

    gap = block_steps[:, None] - block_steps[None, :] - 1.0
    earlier = (gap >= 0).astype(jnp.float32)
    pair_decay = jnp.exp(
        -mode_rates[None, None] * (P_SIZE * jnp.maximum(gap, 0.0))[:, :, None, None]
    ) * earlier[:, :, None, None]
    starts = jnp.sum(pair_decay * block_ends[None], axis=1) + jnp.exp(
        -mode_rates[None] * (P_SIZE * block_steps)[:, None, None]
    ) * incoming[None]
    later_gap = block_steps[None, :] - block_steps[:, None] - 1.0
    later_mask = (later_gap >= 0).astype(jnp.float32)
    later_decay = jnp.exp(
        -mode_rates[None, None] * (P_SIZE * jnp.maximum(later_gap, 0.0))[:, :, None, None]
    ) * later_mask[:, :, None, None]
    ends_back = jnp.sum(later_decay * block_heads[None], axis=1) + jnp.exp(
        -mode_rates[None] * (P_SIZE * (block_count - 1 - block_steps))[:, None, None]
    ) * later_state[None]

    lead = jnp.zeros((block_count, P_SIZE - 1, chan_count), jnp.float32)
    blocks_padded = jnp.concatenate([lead, blocks], 1)
    grads_padded = jnp.concatenate([grad_blocks, lead], 1)
    local_part = sum(
        response[lag][None, None, :] * blocks_padded[:, P_SIZE - 1 - lag : 2 * P_SIZE - 1 - lag]
        for lag in range(P_SIZE)
    )
    carried = jnp.sum(starts[:, :, None, :] * carried_table[None], axis=1)
    long_conv = (local_part + carried).reshape(row_count, chan_count)
    output = (query_part * long_conv).astype(jnp.bfloat16)
    grad_query = (cotangent * long_conv).astype(jnp.bfloat16)

    back_local = sum(
        response[lag][None, None, :] * grads_padded[:, lag : lag + P_SIZE] for lag in range(P_SIZE)
    )
    back_carried = jnp.sum(ends_back[:, :, None, :] * carried_reversed[None], axis=1)
    grad_product = (back_local + back_carried).reshape(row_count, chan_count)
    grad_key = (grad_product * value_part).astype(jnp.bfloat16)
    grad_value = (grad_product * key_part).astype(jnp.bfloat16)

    weighted = jnp.exp(-mode_rates)[None] * block_heads
    cross_part = jnp.sum(weighted * starts, axis=0)
    by_lag = jnp.stack(
        [
            jnp.sum(
                blocks_padded[:, P_SIZE - 1 - lag : 2 * P_SIZE - 1 - lag] * grad_blocks, axis=(0, 1)
            )
            for lag in range(P_SIZE)
        ],
        0,
    )
    local_terms = jnp.sum(by_lag[None] * decay_table, axis=1)

    stacked_half = lax.optimization_barrier(jnp.stack([grad_query, grad_key, grad_value], 0))
    next_rows = passed_along(stacked_half[:, : KS - 1], "ctx", -1)
    stacked = stacked_half.astype(jnp.float32)
    after = jnp.concatenate([stacked, next_rows.astype(jnp.float32)], 1)
    grad_normed = sum(
        (
            short_filters[branch, offset][None, :] * after[branch, offset : offset + row_count]
            for branch in range(3)
            for offset in range(KS)
        )
    )
    short_terms = jnp.stack(
        [
            jnp.einsum(
                "btc,tc->bc",
                stacked_half,
                padded_half[KS - 1 - offset : KS - 1 - offset + row_count],
                preferred_element_type=jnp.float32,
            )
            for offset in range(KS)
        ],
        1,
    )
    partial_sums = jnp.concatenate(
        [cross_part + local_terms, short_terms.reshape(3 * KS, chan_count)], 0
    )
    whole_sums = summed(partial_sums, "ctx")
    norm_factor = 1.0 / jnp.sqrt(jnp.float32(total_rows))
    grad_residues = whole_sums[:M] * norm_factor
    grad_short = whole_sums[M:].reshape(3, KS, chan_count) * norm_factor
    row_dot = summed(jnp.sum(norm_gain[None, :] * grad_normed * stream_wide, axis=1), "ch")
    grad_stream = (
        row_scale[:, None] * norm_gain[None, :] * grad_normed
        - stream_wide * (row_scale**3 * row_dot / total_chans)[:, None]
    ).astype(jnp.bfloat16)
    return (output, grad_stream, grad_residues, grad_short)


def solution(mesh):
    return jax.shard_map(
        per_device,
        mesh=mesh,
        in_specs=(
            P("ctx", "ch"),
            P("ch"),
            P(None, None, "ch"),
            P(None, "ch"),
            P(None, "ch"),
            P("ctx", "ch"),
        ),
        out_specs=(P("ctx", "ch"), P("ctx", "ch"), P(None, "ch"), P(None, None, "ch")),
        check_vma=False,
    )
```

```python
import jax
import jax.numpy as jnp
from jax import lax
from jax.sharding import PartitionSpec as P

M = 16
KS = 3
P_SIZE = 32


EPSILON = 1e-05


def passed_along(value, axis, steps):
    count = lax.axis_size(axis)
    first, last = (max(0, -steps), min(count, count - steps))
    return lax.ppermute(value, axis, [(source, source + steps) for source in range(first, last)])


def radices(count):
    levels = []
    while count > 1:
        radix = 4 if count % 4 == 0 else 2
        levels.append(radix)
        count //= radix
    return levels


PLACES = {}


def hops(first, second):
    rings = PLACES.get("rings")
    return sum(min(abs(a - b), ring - abs(a - b)) for a, b, ring in zip(first, second, rings))


def source_of(target, step, stride, radix, count, flip):
    digit = (target // stride) % radix
    position = (target % stride) ^ flip
    base = target - target % (stride * radix)
    return base + ((digit + step) % radix) * stride + position


def best_flip(axis, step, stride, radix, count):
    places = PLACES.get(axis)
    if places is None or len(places) != count:
        return 0
    best, flip_of_best = None, 0
    for flip in range(stride):
        far = [hops(places[source_of(t, step, stride, radix, count, flip)], places[t]) for t in range(count)]
        score = (max(far), sum(far))
        if best is None or score < best:
            best, flip_of_best = score, flip
    return flip_of_best


def members(value, axis, stride, radix):
    count = lax.axis_size(axis)
    digit = (lax.axis_index(axis) // stride) % radix
    received = [value]
    for step in range(1, radix):
        flip = best_flip(axis, step, stride, radix, count)
        pairs = [(source_of(t, step, stride, radix, count, flip), t) for t in range(count)]
        received.append(lax.ppermute(value, axis, pairs))
    ordered = [
        lax.select_n(((position - digit) % radix).astype(jnp.int32), *received)
        for position in range(radix)
    ]
    return ordered, digit


def power_of_two(count):
    return count & (count - 1) == 0


def entering(own_state, own_back, rates, rows, axis):
    count = lax.axis_size(axis)
    place = lax.axis_index(axis)
    incoming = jnp.zeros_like(own_state)
    later = jnp.zeros_like(own_back)
    totals = jnp.stack([own_state, own_back], 0)
    stride = 1
    for radix in radices(count):
        group, digit = members(totals, axis, stride, radix)
        position = (place % stride).astype(jnp.float32)
        for other in range(radix):
            before = (digit > other).astype(jnp.float32)
            after = (digit < other).astype(jnp.float32)
            ahead = jnp.maximum(digit - 1 - other, 0).astype(jnp.float32) * stride + position
            behind = jnp.maximum(other - 1 - digit, 0).astype(jnp.float32) * stride + (
                stride - 1 - position
            )
            incoming = incoming + before * jnp.exp(-rates * (rows * ahead)) * group[other][0]
            later = later + after * jnp.exp(-rates * (rows * behind)) * group[other][1]
        forward_total = group[0][0]
        backward_total = group[0][1]
        for other in range(1, radix):
            forward_total = (
                jnp.exp(-rates * jnp.float32(rows * stride)) * forward_total + group[other][0]
            )
            backward_total = backward_total + jnp.exp(
                -rates * jnp.float32(rows * stride * other)
            ) * group[other][1]
        totals = jnp.stack([forward_total, backward_total], 0)
        stride *= radix
    return incoming, later


def summed(value, axis):
    count = lax.axis_size(axis)
    if not power_of_two(count):
        return lax.psum(value, axis)
    stride = 1
    for radix in radices(count):
        group, _ = members(value, axis, stride, radix)
        if radix == 4:
            value = (group[0] + group[1]) + (group[2] + group[3])
        else:
            value = group[0] + group[1]
        stride *= radix
    return value


def per_device(stream, norm_gain, short_filters, mode_rates, residues, grad_out):
    row_count, chan_count = stream.shape
    block_count = row_count // P_SIZE
    total_chans = chan_count * lax.axis_size("ch")
    total_rows = row_count * lax.axis_size("ctx")
    stream_wide = stream.astype(jnp.float32)
    rim_rows = passed_along(stream[row_count - (KS - 1) :], "ctx", 1)
    with_rim = jnp.concatenate([rim_rows, stream], 0).astype(jnp.float32)
    squares = summed(jnp.sum(with_rim * with_rim, axis=1), "ch")
    scale_with_rim = lax.rsqrt(squares / total_chans + EPSILON)
    row_scale = scale_with_rim[KS - 1 :]
    padded_half = lax.optimization_barrier(
        (with_rim * scale_with_rim[:, None] * norm_gain[None, :]).astype(jnp.bfloat16)
    )
    padded = padded_half.astype(jnp.float32)
    branches = [
        sum(
            (
                short_filters[branch, offset][None, :]
                * padded[KS - 1 - offset : KS - 1 - offset + row_count]
                for offset in range(KS)
            )
        )
        for branch in range(3)
    ]
    query_part, key_part, value_part = branches
    product = lax.optimization_barrier((key_part * value_part).astype(jnp.bfloat16)).astype(
        jnp.float32
    )
    cotangent = grad_out.astype(jnp.float32)
    grad_conv = cotangent * query_part

    steps = jnp.arange(P_SIZE).astype(jnp.float32)
    decay_table = jnp.exp(-mode_rates[:, None, :] * steps[None, :, None])
    decay_reversed = jnp.exp(-mode_rates[:, None, :] * (P_SIZE - 1.0 - steps)[None, :, None])
    shifted = jnp.exp(-mode_rates[:, None, :] * (steps[None, :, None] + 1.0))
    response = jnp.sum(residues[:, None, :] * decay_table, axis=0)
    carried_table = shifted * residues[:, None, :]
    carried_reversed = (
        jnp.exp(-mode_rates[:, None, :] * (P_SIZE - steps)[None, :, None]) * residues[:, None, :]
    )

    blocks = product.reshape(block_count, P_SIZE, chan_count)
    grad_blocks = grad_conv.reshape(block_count, P_SIZE, chan_count)
    block_ends = jnp.sum(decay_reversed[None] * blocks[:, None], axis=2)
    block_heads = jnp.sum(decay_table[None] * grad_blocks[:, None], axis=2)
    block_steps = jnp.arange(block_count).astype(jnp.float32)
    own_state = jnp.sum(
        jnp.exp(-mode_rates[None] * (P_SIZE * (block_count - 1 - block_steps))[:, None, None])
        * block_ends,
        axis=0,
    )
    own_back = jnp.sum(
        jnp.exp(-mode_rates[None] * (P_SIZE * block_steps)[:, None, None]) * block_heads, axis=0
    )
    incoming, later_state = entering(own_state, own_back, mode_rates, row_count, "ctx")

    gap = block_steps[:, None] - block_steps[None, :] - 1.0
    earlier = (gap >= 0).astype(jnp.float32)
    pair_decay = jnp.exp(
        -mode_rates[None, None] * (P_SIZE * jnp.maximum(gap, 0.0))[:, :, None, None]
    ) * earlier[:, :, None, None]
    starts = jnp.sum(pair_decay * block_ends[None], axis=1) + jnp.exp(
        -mode_rates[None] * (P_SIZE * block_steps)[:, None, None]
    ) * incoming[None]
    later_gap = block_steps[None, :] - block_steps[:, None] - 1.0
    later_mask = (later_gap >= 0).astype(jnp.float32)
    later_decay = jnp.exp(
        -mode_rates[None, None] * (P_SIZE * jnp.maximum(later_gap, 0.0))[:, :, None, None]
    ) * later_mask[:, :, None, None]
    ends_back = jnp.sum(later_decay * block_heads[None], axis=1) + jnp.exp(
        -mode_rates[None] * (P_SIZE * (block_count - 1 - block_steps))[:, None, None]
    ) * later_state[None]

    lead = jnp.zeros((block_count, P_SIZE - 1, chan_count), jnp.float32)
    blocks_padded = jnp.concatenate([lead, blocks], 1)
    grads_padded = jnp.concatenate([grad_blocks, lead], 1)
    local_part = sum(
        response[lag][None, None, :] * blocks_padded[:, P_SIZE - 1 - lag : 2 * P_SIZE - 1 - lag]
        for lag in range(P_SIZE)
    )
    carried = jnp.sum(starts[:, :, None, :] * carried_table[None], axis=1)
    long_conv = (local_part + carried).reshape(row_count, chan_count)
    output = (query_part * long_conv).astype(jnp.bfloat16)
    grad_query = (cotangent * long_conv).astype(jnp.bfloat16)

    back_local = sum(
        response[lag][None, None, :] * grads_padded[:, lag : lag + P_SIZE] for lag in range(P_SIZE)
    )
    back_carried = jnp.sum(ends_back[:, :, None, :] * carried_reversed[None], axis=1)
    grad_product = (back_local + back_carried).reshape(row_count, chan_count)
    grad_key = (grad_product * value_part).astype(jnp.bfloat16)
    grad_value = (grad_product * key_part).astype(jnp.bfloat16)

    weighted = jnp.exp(-mode_rates)[None] * block_heads
    cross_part = jnp.sum(weighted * starts, axis=0)
    by_lag = jnp.stack(
        [
            jnp.sum(
                blocks_padded[:, P_SIZE - 1 - lag : 2 * P_SIZE - 1 - lag] * grad_blocks, axis=(0, 1)
            )
            for lag in range(P_SIZE)
        ],
        0,
    )
    local_terms = jnp.sum(by_lag[None] * decay_table, axis=1)

    stacked_half = lax.optimization_barrier(jnp.stack([grad_query, grad_key, grad_value], 0))
    next_rows = passed_along(stacked_half[:, : KS - 1], "ctx", -1)
    stacked = stacked_half.astype(jnp.float32)
    after = jnp.concatenate([stacked, next_rows.astype(jnp.float32)], 1)
    grad_normed = sum(
        (
            short_filters[branch, offset][None, :] * after[branch, offset : offset + row_count]
            for branch in range(3)
            for offset in range(KS)
        )
    )
    short_terms = jnp.stack(
        [
            jnp.einsum(
                "btc,tc->bc",
                stacked_half,
                padded_half[KS - 1 - offset : KS - 1 - offset + row_count],
                preferred_element_type=jnp.float32,
            )
            for offset in range(KS)
        ],
        1,
    )
    partial_sums = jnp.concatenate(
        [cross_part + local_terms, short_terms.reshape(3 * KS, chan_count)], 0
    )
    whole_sums = summed(partial_sums, "ctx")
    norm_factor = 1.0 / jnp.sqrt(jnp.float32(total_rows))
    grad_residues = whole_sums[:M] * norm_factor
    grad_short = whole_sums[M:].reshape(3, KS, chan_count) * norm_factor
    row_dot = summed(jnp.sum(norm_gain[None, :] * grad_normed * stream_wide, axis=1), "ch")
    grad_stream = (
        row_scale[:, None] * norm_gain[None, :] * grad_normed
        - stream_wide * (row_scale**3 * row_dot / total_chans)[:, None]
    ).astype(jnp.bfloat16)
    return (output, grad_stream, grad_residues, grad_short)


def solution(mesh):
    devices = mesh.devices
    if all(hasattr(d, "coords") for d in devices.flat):
        coords = [tuple(d.coords) for d in devices.flat]
        PLACES["rings"] = tuple(max(c[k] for c in coords) + 1 for k in range(len(coords[0])))
        PLACES["ctx"] = [tuple(d.coords) for d in devices[:, 0]]
        PLACES["ch"] = [tuple(d.coords) for d in devices[0, :]]
    return jax.shard_map(
        per_device,
        mesh=mesh,
        in_specs=(
            P("ctx", "ch"),
            P("ch"),
            P(None, None, "ch"),
            P(None, "ch"),
            P(None, "ch"),
            P("ctx", "ch"),
        ),
        out_specs=(P("ctx", "ch"), P("ctx", "ch"), P(None, "ch"), P(None, None, "ch")),
        check_vma=False,
    )
```

```python
import jax
import jax.numpy as jnp
from jax import lax
from jax.sharding import PartitionSpec as P

M = 16
KS = 3
P_SIZE = 32


EPSILON = 1e-05


def passed_along(value, axis, steps):
    count = lax.axis_size(axis)
    first, last = (max(0, -steps), min(count, count - steps))
    return lax.ppermute(value, axis, [(source, source + steps) for source in range(first, last)])


def radices(count):
    levels = []
    while count > 1:
        radix = 4 if count % 4 == 0 else 2
        levels.append(radix)
        count //= radix
    return levels


PLACES = {}


def hops(first, second):
    rings = PLACES.get("rings")
    return sum(min(abs(a - b), ring - abs(a - b)) for a, b, ring in zip(first, second, rings))


def source_of(target, step, stride, radix, count, flip):
    digit = (target // stride) % radix
    position = (target % stride) ^ flip
    base = target - target % (stride * radix)
    return base + ((digit + step) % radix) * stride + position


def best_flip(axis, step, stride, radix, count):
    places = PLACES.get(axis)
    if places is None or len(places) != count:
        return 0
    best, flip_of_best = None, 0
    for flip in range(stride):
        far = [hops(places[source_of(t, step, stride, radix, count, flip)], places[t]) for t in range(count)]
        score = (max(far), sum(far))
        if best is None or score < best:
            best, flip_of_best = score, flip
    return flip_of_best


def members(value, axis, stride, radix):
    count = lax.axis_size(axis)
    digit = (lax.axis_index(axis) // stride) % radix
    received = [value]
    for step in range(1, radix):
        flip = best_flip(axis, step, stride, radix, count)
        pairs = [(source_of(t, step, stride, radix, count, flip), t) for t in range(count)]
        received.append(lax.ppermute(value, axis, pairs))
    ordered = [
        lax.select_n(((position - digit) % radix).astype(jnp.int32), *received)
        for position in range(radix)
    ]
    return ordered, digit


def power_of_two(count):
    return count & (count - 1) == 0


def entering(own_state, own_back, rates, rows, axis, riders):
    count = lax.axis_size(axis)
    place = lax.axis_index(axis)
    incoming = jnp.zeros_like(own_state)
    later = jnp.zeros_like(own_back)
    totals = jnp.stack([own_state, own_back], 0)
    stride = 1
    for radix in radices(count):
        group, digit = members(totals, axis, stride, radix)
        if stride == 1:
            group, riders = lax.optimization_barrier((group, riders))
        position = (place % stride).astype(jnp.float32)
        for other in range(radix):
            before = (digit > other).astype(jnp.float32)
            after = (digit < other).astype(jnp.float32)
            ahead = jnp.maximum(digit - 1 - other, 0).astype(jnp.float32) * stride + position
            behind = jnp.maximum(other - 1 - digit, 0).astype(jnp.float32) * stride + (
                stride - 1 - position
            )
            incoming = incoming + before * jnp.exp(-rates * (rows * ahead)) * group[other][0]
            later = later + after * jnp.exp(-rates * (rows * behind)) * group[other][1]
        forward_total = group[0][0]
        backward_total = group[0][1]
        for other in range(1, radix):
            forward_total = (
                jnp.exp(-rates * jnp.float32(rows * stride)) * forward_total + group[other][0]
            )
            backward_total = backward_total + jnp.exp(
                -rates * jnp.float32(rows * stride * other)
            ) * group[other][1]
        totals = jnp.stack([forward_total, backward_total], 0)
        stride *= radix
    return incoming, later, riders


def summed(value, axis):
    count = lax.axis_size(axis)
    if not power_of_two(count):
        return lax.psum(value, axis)
    stride = 1
    for radix in radices(count):
        group, _ = members(value, axis, stride, radix)
        if radix == 4:
            value = (group[0] + group[1]) + (group[2] + group[3])
        else:
            value = group[0] + group[1]
        stride *= radix
    return value


def per_device(stream, norm_gain, short_filters, mode_rates, residues, grad_out):
    row_count, chan_count = stream.shape
    block_count = row_count // P_SIZE
    total_chans = chan_count * lax.axis_size("ch")
    total_rows = row_count * lax.axis_size("ctx")
    stream_wide = stream.astype(jnp.float32)
    rim_rows = passed_along(stream[row_count - (KS - 1) :], "ctx", 1)
    with_rim = jnp.concatenate([rim_rows, stream], 0).astype(jnp.float32)
    squares = summed(jnp.sum(with_rim * with_rim, axis=1), "ch")
    scale_with_rim = lax.rsqrt(squares / total_chans + EPSILON)
    row_scale = scale_with_rim[KS - 1 :]
    padded_half = lax.optimization_barrier(
        (with_rim * scale_with_rim[:, None] * norm_gain[None, :]).astype(jnp.bfloat16)
    )
    padded = padded_half.astype(jnp.float32)
    branches = [
        sum(
            (
                short_filters[branch, offset][None, :]
                * padded[KS - 1 - offset : KS - 1 - offset + row_count]
                for offset in range(KS)
            )
        )
        for branch in range(3)
    ]
    query_part, key_part, value_part = branches
    product = lax.optimization_barrier((key_part * value_part).astype(jnp.bfloat16)).astype(
        jnp.float32
    )
    cotangent = grad_out.astype(jnp.float32)
    grad_conv = cotangent * query_part

    steps = jnp.arange(P_SIZE).astype(jnp.float32)
    decay_table = jnp.exp(-mode_rates[:, None, :] * steps[None, :, None])
    decay_reversed = jnp.exp(-mode_rates[:, None, :] * (P_SIZE - 1.0 - steps)[None, :, None])
    shifted = jnp.exp(-mode_rates[:, None, :] * (steps[None, :, None] + 1.0))
    response = jnp.sum(residues[:, None, :] * decay_table, axis=0)
    carried_table = shifted * residues[:, None, :]
    carried_reversed = (
        jnp.exp(-mode_rates[:, None, :] * (P_SIZE - steps)[None, :, None]) * residues[:, None, :]
    )

    blocks = product.reshape(block_count, P_SIZE, chan_count)
    grad_blocks = grad_conv.reshape(block_count, P_SIZE, chan_count)
    block_ends = jnp.sum(decay_reversed[None] * blocks[:, None], axis=2)
    block_heads = jnp.sum(decay_table[None] * grad_blocks[:, None], axis=2)
    block_steps = jnp.arange(block_count).astype(jnp.float32)
    own_state = jnp.sum(
        jnp.exp(-mode_rates[None] * (P_SIZE * (block_count - 1 - block_steps))[:, None, None])
        * block_ends,
        axis=0,
    )
    own_back = jnp.sum(
        jnp.exp(-mode_rates[None] * (P_SIZE * block_steps)[:, None, None]) * block_heads, axis=0
    )
    lead = jnp.zeros((block_count, P_SIZE - 1, chan_count), jnp.float32)
    incoming, later_state, (late_blocks, late_grads) = entering(
        own_state, own_back, mode_rates, row_count, "ctx", (blocks, grad_blocks)
    )
    late_padded = jnp.concatenate([lead, late_blocks], 1)

    gap = block_steps[:, None] - block_steps[None, :] - 1.0
    earlier = (gap >= 0).astype(jnp.float32)
    pair_decay = jnp.exp(
        -mode_rates[None, None] * (P_SIZE * jnp.maximum(gap, 0.0))[:, :, None, None]
    ) * earlier[:, :, None, None]
    starts = jnp.sum(pair_decay * block_ends[None], axis=1) + jnp.exp(
        -mode_rates[None] * (P_SIZE * block_steps)[:, None, None]
    ) * incoming[None]
    later_gap = block_steps[None, :] - block_steps[:, None] - 1.0
    later_mask = (later_gap >= 0).astype(jnp.float32)
    later_decay = jnp.exp(
        -mode_rates[None, None] * (P_SIZE * jnp.maximum(later_gap, 0.0))[:, :, None, None]
    ) * later_mask[:, :, None, None]
    ends_back = jnp.sum(later_decay * block_heads[None], axis=1) + jnp.exp(
        -mode_rates[None] * (P_SIZE * (block_count - 1 - block_steps))[:, None, None]
    ) * later_state[None]

    lead = jnp.zeros((block_count, P_SIZE - 1, chan_count), jnp.float32)
    blocks_padded = jnp.concatenate([lead, blocks], 1)
    grads_padded = jnp.concatenate([grad_blocks, lead], 1)
    local_part = sum(
        response[lag][None, None, :] * blocks_padded[:, P_SIZE - 1 - lag : 2 * P_SIZE - 1 - lag]
        for lag in range(P_SIZE)
    )
    carried = jnp.sum(starts[:, :, None, :] * carried_table[None], axis=1)
    long_conv = (local_part + carried).reshape(row_count, chan_count)
    output = (query_part * long_conv).astype(jnp.bfloat16)
    grad_query = (cotangent * long_conv).astype(jnp.bfloat16)

    back_local = sum(
        response[lag][None, None, :] * grads_padded[:, lag : lag + P_SIZE] for lag in range(P_SIZE)
    )
    back_carried = jnp.sum(ends_back[:, :, None, :] * carried_reversed[None], axis=1)
    grad_product = (back_local + back_carried).reshape(row_count, chan_count)
    grad_key = (grad_product * value_part).astype(jnp.bfloat16)
    grad_value = (grad_product * key_part).astype(jnp.bfloat16)

    weighted = jnp.exp(-mode_rates)[None] * block_heads
    cross_part = jnp.sum(weighted * starts, axis=0)
    by_lag = jnp.stack(
        [
            jnp.sum(
                late_padded[:, P_SIZE - 1 - lag : 2 * P_SIZE - 1 - lag] * late_grads, axis=(0, 1)
            )
            for lag in range(P_SIZE)
        ],
        0,
    )
    local_terms = jnp.sum(by_lag[None] * decay_table, axis=1)

    stacked_half = lax.optimization_barrier(jnp.stack([grad_query, grad_key, grad_value], 0))
    next_rows = passed_along(stacked_half[:, : KS - 1], "ctx", -1)
    stacked = stacked_half.astype(jnp.float32)
    after = jnp.concatenate([stacked, next_rows.astype(jnp.float32)], 1)
    grad_normed = sum(
        (
            short_filters[branch, offset][None, :] * after[branch, offset : offset + row_count]
            for branch in range(3)
            for offset in range(KS)
        )
    )
    short_terms = jnp.stack(
        [
            jnp.einsum(
                "btc,tc->bc",
                stacked_half,
                padded_half[KS - 1 - offset : KS - 1 - offset + row_count],
                preferred_element_type=jnp.float32,
            )
            for offset in range(KS)
        ],
        1,
    )
    partial_sums = jnp.concatenate(
        [cross_part + local_terms, short_terms.reshape(3 * KS, chan_count)], 0
    )
    whole_sums = summed(partial_sums, "ctx")
    norm_factor = 1.0 / jnp.sqrt(jnp.float32(total_rows))
    grad_residues = whole_sums[:M] * norm_factor
    grad_short = whole_sums[M:].reshape(3, KS, chan_count) * norm_factor
    row_dot = summed(jnp.sum(norm_gain[None, :] * grad_normed * stream_wide, axis=1), "ch")
    grad_stream = (
        row_scale[:, None] * norm_gain[None, :] * grad_normed
        - stream_wide * (row_scale**3 * row_dot / total_chans)[:, None]
    ).astype(jnp.bfloat16)
    return (output, grad_stream, grad_residues, grad_short)


def solution(mesh):
    devices = mesh.devices
    if all(hasattr(d, "coords") for d in devices.flat):
        coords = [tuple(d.coords) for d in devices.flat]
        PLACES["rings"] = tuple(max(c[k] for c in coords) + 1 for k in range(len(coords[0])))
        PLACES["ctx"] = [tuple(d.coords) for d in devices[:, 0]]
        PLACES["ch"] = [tuple(d.coords) for d in devices[0, :]]
    return jax.shard_map(
        per_device,
        mesh=mesh,
        in_specs=(
            P("ctx", "ch"),
            P("ch"),
            P(None, None, "ch"),
            P(None, "ch"),
            P(None, "ch"),
            P("ctx", "ch"),
        ),
        out_specs=(P("ctx", "ch"), P("ctx", "ch"), P(None, "ch"), P(None, None, "ch")),
        check_vma=False,
    )
```

```python
import jax
import jax.numpy as jnp
from jax import lax
from jax.sharding import PartitionSpec as P

M = 16
KS = 3
P_SIZE = 32


EPSILON = 1e-05


def passed_along(value, axis, steps):
    count = lax.axis_size(axis)
    first, last = (max(0, -steps), min(count, count - steps))
    return lax.ppermute(value, axis, [(source, source + steps) for source in range(first, last)])


def radices(count):
    levels = []
    while count > 1:
        radix = 4 if count % 4 == 0 else 2
        levels.append(radix)
        count //= radix
    return levels


PLACES = {}


def hops(first, second):
    rings = PLACES.get("rings")
    return sum(min(abs(a - b), ring - abs(a - b)) for a, b, ring in zip(first, second, rings))


def source_of(target, step, stride, radix, count, flip):
    digit = (target // stride) % radix
    position = (target % stride) ^ flip
    base = target - target % (stride * radix)
    return base + ((digit + step) % radix) * stride + position


def best_flip(axis, step, stride, radix, count):
    places = PLACES.get(axis)
    if places is None or len(places) != count:
        return 0
    best, flip_of_best = None, 0
    for flip in range(stride):
        far = [hops(places[source_of(t, step, stride, radix, count, flip)], places[t]) for t in range(count)]
        score = (max(far), sum(far))
        if best is None or score < best:
            best, flip_of_best = score, flip
    return flip_of_best


def members(value, axis, stride, radix):
    count = lax.axis_size(axis)
    digit = (lax.axis_index(axis) // stride) % radix
    received = [value]
    for step in range(1, radix):
        flip = best_flip(axis, step, stride, radix, count)
        pairs = [(source_of(t, step, stride, radix, count, flip), t) for t in range(count)]
        received.append(lax.ppermute(value, axis, pairs))
    ordered = [
        lax.select_n(((position - digit) % radix).astype(jnp.int32), *received)
        for position in range(radix)
    ]
    return ordered, digit


def power_of_two(count):
    return count & (count - 1) == 0


def entering(own_state, own_back, rates, rows, axis, riders):
    count = lax.axis_size(axis)
    place = lax.axis_index(axis)
    incoming = jnp.zeros_like(own_state)
    later = jnp.zeros_like(own_back)
    totals = jnp.stack([own_state, own_back], 0)
    stride = 1
    for radix in radices(count):
        group, digit = members(totals, axis, stride, radix)
        if stride == 1:
            group, riders = lax.optimization_barrier((group, riders))
        position = (place % stride).astype(jnp.float32)
        for other in range(radix):
            before = (digit > other).astype(jnp.float32)
            after = (digit < other).astype(jnp.float32)
            ahead = jnp.maximum(digit - 1 - other, 0).astype(jnp.float32) * stride + position
            behind = jnp.maximum(other - 1 - digit, 0).astype(jnp.float32) * stride + (
                stride - 1 - position
            )
            incoming = incoming + before * jnp.exp(-rates * (rows * ahead)) * group[other][0]
            later = later + after * jnp.exp(-rates * (rows * behind)) * group[other][1]
        forward_total = group[0][0]
        backward_total = group[0][1]
        for other in range(1, radix):
            forward_total = (
                jnp.exp(-rates * jnp.float32(rows * stride)) * forward_total + group[other][0]
            )
            backward_total = backward_total + jnp.exp(
                -rates * jnp.float32(rows * stride * other)
            ) * group[other][1]
        totals = jnp.stack([forward_total, backward_total], 0)
        stride *= radix
    return incoming, later, riders


def summed(value, axis):
    count = lax.axis_size(axis)
    if not power_of_two(count):
        return lax.psum(value, axis)
    stride = 1
    for radix in radices(count):
        group, _ = members(value, axis, stride, radix)
        if radix == 4:
            value = (group[0] + group[1]) + (group[2] + group[3])
        else:
            value = group[0] + group[1]
        stride *= radix
    return value


def per_device(stream, norm_gain, short_filters, mode_rates, residues, grad_out):
    row_count, chan_count = stream.shape
    block_count = row_count // P_SIZE
    total_chans = chan_count * lax.axis_size("ch")
    total_rows = row_count * lax.axis_size("ctx")
    stream_wide = stream.astype(jnp.float32)
    ch_count = lax.axis_size("ch")
    ctx_count = lax.axis_size("ctx")
    ch_place = lax.axis_index("ch")
    rim_raw = stream[row_count - (KS - 1) :]
    shards = []
    for step in range(ch_count):
        pairs = [
            ((place - 1) * ch_count + (shard + step) % ch_count, place * ch_count + shard)
            for place in range(1, ctx_count)
            for shard in range(ch_count)
        ]
        shards.append(lax.ppermute(rim_raw, ("ctx", "ch"), pairs))
    shard_sums = [jnp.sum(jnp.square(s.astype(jnp.float32)), axis=1) for s in shards]
    ordered = [
        lax.select_n(((position - ch_place) % ch_count).astype(jnp.int32), *shard_sums)
        for position in range(ch_count)
    ]
    while len(ordered) > 1:
        radix = radices(len(ordered))[0]
        ordered = [
            (ordered[i] + ordered[i + 1]) + (ordered[i + 2] + ordered[i + 3])
            if radix == 4
            else ordered[i] + ordered[i + 1]
            for i in range(0, len(ordered), radix)
        ]
    rim_squares = ordered[0]
    rim_scale = lax.rsqrt(rim_squares / total_chans + EPSILON)
    squares = summed(jnp.sum(stream_wide * stream_wide, axis=1), "ch")
    row_scale = lax.rsqrt(squares / total_chans + EPSILON)
    with_rim = jnp.concatenate([shards[0].astype(jnp.float32), stream_wide], 0)
    scale_with_rim = jnp.concatenate([rim_scale, row_scale], 0)
    padded_half = lax.optimization_barrier(
        (with_rim * scale_with_rim[:, None] * norm_gain[None, :]).astype(jnp.bfloat16)
    )
    padded = padded_half.astype(jnp.float32)
    branches = [
        sum(
            (
                short_filters[branch, offset][None, :]
                * padded[KS - 1 - offset : KS - 1 - offset + row_count]
                for offset in range(KS)
            )
        )
        for branch in range(3)
    ]
    query_part, key_part, value_part = branches
    product = lax.optimization_barrier((key_part * value_part).astype(jnp.bfloat16)).astype(
        jnp.float32
    )
    cotangent = grad_out.astype(jnp.float32)
    grad_conv = cotangent * query_part

    steps = jnp.arange(P_SIZE).astype(jnp.float32)
    decay_table = jnp.exp(-mode_rates[:, None, :] * steps[None, :, None])
    decay_reversed = jnp.exp(-mode_rates[:, None, :] * (P_SIZE - 1.0 - steps)[None, :, None])
    shifted = jnp.exp(-mode_rates[:, None, :] * (steps[None, :, None] + 1.0))
    response = jnp.sum(residues[:, None, :] * decay_table, axis=0)
    carried_table = shifted * residues[:, None, :]
    carried_reversed = (
        jnp.exp(-mode_rates[:, None, :] * (P_SIZE - steps)[None, :, None]) * residues[:, None, :]
    )

    blocks = product.reshape(block_count, P_SIZE, chan_count)
    grad_blocks = grad_conv.reshape(block_count, P_SIZE, chan_count)
    block_ends = jnp.sum(decay_reversed[None] * blocks[:, None], axis=2)
    block_heads = jnp.sum(decay_table[None] * grad_blocks[:, None], axis=2)
    block_steps = jnp.arange(block_count).astype(jnp.float32)
    own_state = jnp.sum(
        jnp.exp(-mode_rates[None] * (P_SIZE * (block_count - 1 - block_steps))[:, None, None])
        * block_ends,
        axis=0,
    )
    own_back = jnp.sum(
        jnp.exp(-mode_rates[None] * (P_SIZE * block_steps)[:, None, None]) * block_heads, axis=0
    )
    lead = jnp.zeros((block_count, P_SIZE - 1, chan_count), jnp.float32)
    incoming, later_state, (late_blocks, late_grads) = entering(
        own_state, own_back, mode_rates, row_count, "ctx", (blocks, grad_blocks)
    )
    late_padded = jnp.concatenate([lead, late_blocks], 1)

    gap = block_steps[:, None] - block_steps[None, :] - 1.0
    earlier = (gap >= 0).astype(jnp.float32)
    pair_decay = jnp.exp(
        -mode_rates[None, None] * (P_SIZE * jnp.maximum(gap, 0.0))[:, :, None, None]
    ) * earlier[:, :, None, None]
    starts = jnp.sum(pair_decay * block_ends[None], axis=1) + jnp.exp(
        -mode_rates[None] * (P_SIZE * block_steps)[:, None, None]
    ) * incoming[None]
    later_gap = block_steps[None, :] - block_steps[:, None] - 1.0
    later_mask = (later_gap >= 0).astype(jnp.float32)
    later_decay = jnp.exp(
        -mode_rates[None, None] * (P_SIZE * jnp.maximum(later_gap, 0.0))[:, :, None, None]
    ) * later_mask[:, :, None, None]
    ends_back = jnp.sum(later_decay * block_heads[None], axis=1) + jnp.exp(
        -mode_rates[None] * (P_SIZE * (block_count - 1 - block_steps))[:, None, None]
    ) * later_state[None]

    lead = jnp.zeros((block_count, P_SIZE - 1, chan_count), jnp.float32)
    blocks_padded = jnp.concatenate([lead, blocks], 1)
    grads_padded = jnp.concatenate([grad_blocks, lead], 1)
    local_part = sum(
        response[lag][None, None, :] * blocks_padded[:, P_SIZE - 1 - lag : 2 * P_SIZE - 1 - lag]
        for lag in range(P_SIZE)
    )
    carried = jnp.sum(starts[:, :, None, :] * carried_table[None], axis=1)
    long_conv = (local_part + carried).reshape(row_count, chan_count)
    output = (query_part * long_conv).astype(jnp.bfloat16)
    grad_query = (cotangent * long_conv).astype(jnp.bfloat16)

    back_local = sum(
        response[lag][None, None, :] * grads_padded[:, lag : lag + P_SIZE] for lag in range(P_SIZE)
    )
    back_carried = jnp.sum(ends_back[:, :, None, :] * carried_reversed[None], axis=1)
    grad_product = (back_local + back_carried).reshape(row_count, chan_count)
    grad_key = (grad_product * value_part).astype(jnp.bfloat16)
    grad_value = (grad_product * key_part).astype(jnp.bfloat16)

    weighted = jnp.exp(-mode_rates)[None] * block_heads
    cross_part = jnp.sum(weighted * starts, axis=0)
    by_lag = jnp.stack(
        [
            jnp.sum(
                late_padded[:, P_SIZE - 1 - lag : 2 * P_SIZE - 1 - lag] * late_grads, axis=(0, 1)
            )
            for lag in range(P_SIZE)
        ],
        0,
    )
    local_terms = jnp.sum(by_lag[None] * decay_table, axis=1)

    stacked_half = lax.optimization_barrier(jnp.stack([grad_query, grad_key, grad_value], 0))
    next_rows = passed_along(stacked_half[:, : KS - 1], "ctx", -1)
    stacked = stacked_half.astype(jnp.float32)
    after = jnp.concatenate([stacked, next_rows.astype(jnp.float32)], 1)
    grad_normed = sum(
        (
            short_filters[branch, offset][None, :] * after[branch, offset : offset + row_count]
            for branch in range(3)
            for offset in range(KS)
        )
    )
    short_terms = jnp.stack(
        [
            jnp.einsum(
                "btc,tc->bc",
                stacked_half,
                padded_half[KS - 1 - offset : KS - 1 - offset + row_count],
                preferred_element_type=jnp.float32,
            )
            for offset in range(KS)
        ],
        1,
    )
    partial_sums = jnp.concatenate(
        [cross_part + local_terms, short_terms.reshape(3 * KS, chan_count)], 0
    )
    whole_sums = summed(partial_sums, "ctx")
    norm_factor = 1.0 / jnp.sqrt(jnp.float32(total_rows))
    grad_residues = whole_sums[:M] * norm_factor
    grad_short = whole_sums[M:].reshape(3, KS, chan_count) * norm_factor
    row_dot = summed(jnp.sum(norm_gain[None, :] * grad_normed * stream_wide, axis=1), "ch")
    grad_stream = (
        row_scale[:, None] * norm_gain[None, :] * grad_normed
        - stream_wide * (row_scale**3 * row_dot / total_chans)[:, None]
    ).astype(jnp.bfloat16)
    return (output, grad_stream, grad_residues, grad_short)


def solution(mesh):
    devices = mesh.devices
    if all(hasattr(d, "coords") for d in devices.flat):
        coords = [tuple(d.coords) for d in devices.flat]
        PLACES["rings"] = tuple(max(c[k] for c in coords) + 1 for k in range(len(coords[0])))
        PLACES["ctx"] = [tuple(d.coords) for d in devices[:, 0]]
        PLACES["ch"] = [tuple(d.coords) for d in devices[0, :]]
    return jax.shard_map(
        per_device,
        mesh=mesh,
        in_specs=(
            P("ctx", "ch"),
            P("ch"),
            P(None, None, "ch"),
            P(None, "ch"),
            P(None, "ch"),
            P("ctx", "ch"),
        ),
        out_specs=(P("ctx", "ch"), P("ctx", "ch"), P(None, "ch"), P(None, None, "ch")),
        check_vma=False,
    )
```

```python
import jax
import jax.numpy as jnp
from jax import lax
from jax.sharding import PartitionSpec as P

M = 16
KS = 3
P_SIZE = 32


EPSILON = 1e-05


def passed_along(value, axis, steps):
    count = lax.axis_size(axis)
    first, last = (max(0, -steps), min(count, count - steps))
    return lax.ppermute(value, axis, [(source, source + steps) for source in range(first, last)])


def radices(count):
    levels = []
    while count > 1:
        radix = 4 if count % 4 == 0 else 2
        levels.append(radix)
        count //= radix
    return levels


PLACES = {}


def hops(first, second):
    rings = PLACES.get("rings")
    return sum(min(abs(a - b), ring - abs(a - b)) for a, b, ring in zip(first, second, rings))


def source_of(target, step, stride, radix, count, flip):
    digit = (target // stride) % radix
    position = (target % stride) ^ flip
    base = target - target % (stride * radix)
    return base + ((digit + step) % radix) * stride + position


def best_flip(axis, step, stride, radix, count):
    places = PLACES.get(axis)
    if places is None or len(places) != count:
        return 0
    best, flip_of_best = None, 0
    for flip in range(stride):
        far = [hops(places[source_of(t, step, stride, radix, count, flip)], places[t]) for t in range(count)]
        score = (max(far), sum(far))
        if best is None or score < best:
            best, flip_of_best = score, flip
    return flip_of_best


def members(value, axis, stride, radix):
    count = lax.axis_size(axis)
    digit = (lax.axis_index(axis) // stride) % radix
    received = [value]
    for step in range(1, radix):
        flip = best_flip(axis, step, stride, radix, count)
        pairs = [(source_of(t, step, stride, radix, count, flip), t) for t in range(count)]
        received.append(lax.ppermute(value, axis, pairs))
    ordered = [
        lax.select_n(((position - digit) % radix).astype(jnp.int32), *received)
        for position in range(radix)
    ]
    return ordered, digit


def power_of_two(count):
    return count & (count - 1) == 0


def entering(own_state, own_back, rates, rows, axis, riders, work):
    count = lax.axis_size(axis)
    place = lax.axis_index(axis)
    incoming = jnp.zeros_like(own_state)
    later = jnp.zeros_like(own_back)
    totals = jnp.stack([own_state, own_back], 0)
    stride = 1
    for radix in radices(count):
        group, digit = members(totals, axis, stride, radix)
        if stride == 1:
            _, riders = lax.optimization_barrier((group, riders))
            riders = work(*riders)
        position = (place % stride).astype(jnp.float32)
        for other in range(radix):
            before = (digit > other).astype(jnp.float32)
            after = (digit < other).astype(jnp.float32)
            ahead = jnp.maximum(digit - 1 - other, 0).astype(jnp.float32) * stride + position
            behind = jnp.maximum(other - 1 - digit, 0).astype(jnp.float32) * stride + (
                stride - 1 - position
            )
            incoming = incoming + before * jnp.exp(-rates * (rows * ahead)) * group[other][0]
            later = later + after * jnp.exp(-rates * (rows * behind)) * group[other][1]
        forward_total = group[0][0]
        backward_total = group[0][1]
        for other in range(1, radix):
            forward_total = (
                jnp.exp(-rates * jnp.float32(rows * stride)) * forward_total + group[other][0]
            )
            backward_total = backward_total + jnp.exp(
                -rates * jnp.float32(rows * stride * other)
            ) * group[other][1]
        totals = jnp.stack([forward_total, backward_total], 0)
        stride *= radix
    return lax.optimization_barrier((incoming, later, riders))


def summed(value, axis):
    count = lax.axis_size(axis)
    if not power_of_two(count):
        return lax.psum(value, axis)
    stride = 1
    for radix in radices(count):
        group, _ = members(value, axis, stride, radix)
        if radix == 4:
            value = (group[0] + group[1]) + (group[2] + group[3])
        else:
            value = group[0] + group[1]
        stride *= radix
    return value


def per_device(stream, norm_gain, short_filters, mode_rates, residues, grad_out):
    row_count, chan_count = stream.shape
    block_count = row_count // P_SIZE
    total_chans = chan_count * lax.axis_size("ch")
    total_rows = row_count * lax.axis_size("ctx")
    stream_wide = stream.astype(jnp.float32)
    rim_rows = passed_along(stream[row_count - (KS - 1) :], "ctx", 1)
    with_rim = jnp.concatenate([rim_rows, stream], 0).astype(jnp.float32)
    squares = summed(jnp.sum(with_rim * with_rim, axis=1), "ch")
    scale_with_rim = lax.rsqrt(squares / total_chans + EPSILON)
    row_scale = scale_with_rim[KS - 1 :]
    padded_half = lax.optimization_barrier(
        (with_rim * scale_with_rim[:, None] * norm_gain[None, :]).astype(jnp.bfloat16)
    )
    padded = padded_half.astype(jnp.float32)
    branches = [
        sum(
            (
                short_filters[branch, offset][None, :]
                * padded[KS - 1 - offset : KS - 1 - offset + row_count]
                for offset in range(KS)
            )
        )
        for branch in range(3)
    ]
    query_part, key_part, value_part = branches
    product = lax.optimization_barrier((key_part * value_part).astype(jnp.bfloat16)).astype(
        jnp.float32
    )
    cotangent = grad_out.astype(jnp.float32)
    grad_conv = cotangent * query_part

    steps = jnp.arange(P_SIZE).astype(jnp.float32)
    decay_table = jnp.exp(-mode_rates[:, None, :] * steps[None, :, None])
    decay_reversed = jnp.exp(-mode_rates[:, None, :] * (P_SIZE - 1.0 - steps)[None, :, None])
    shifted = jnp.exp(-mode_rates[:, None, :] * (steps[None, :, None] + 1.0))
    response = jnp.sum(residues[:, None, :] * decay_table, axis=0)
    carried_table = shifted * residues[:, None, :]
    carried_reversed = (
        jnp.exp(-mode_rates[:, None, :] * (P_SIZE - steps)[None, :, None]) * residues[:, None, :]
    )

    blocks = product.reshape(block_count, P_SIZE, chan_count)
    grad_blocks = grad_conv.reshape(block_count, P_SIZE, chan_count)
    block_ends = jnp.sum(decay_reversed[None] * blocks[:, None], axis=2)
    block_heads = jnp.sum(decay_table[None] * grad_blocks[:, None], axis=2)
    block_steps = jnp.arange(block_count).astype(jnp.float32)
    own_state = jnp.sum(
        jnp.exp(-mode_rates[None] * (P_SIZE * (block_count - 1 - block_steps))[:, None, None])
        * block_ends,
        axis=0,
    )
    own_back = jnp.sum(
        jnp.exp(-mode_rates[None] * (P_SIZE * block_steps)[:, None, None]) * block_heads, axis=0
    )
    lead = jnp.zeros((block_count, P_SIZE - 1, chan_count), jnp.float32)

    def local_work(some_blocks, some_grads):
        blocks_padded = jnp.concatenate([lead, some_blocks], 1)
        grads_padded = jnp.concatenate([some_grads, lead], 1)
        local_part = sum(
            response[lag][None, None, :]
            * blocks_padded[:, P_SIZE - 1 - lag : 2 * P_SIZE - 1 - lag]
            for lag in range(P_SIZE)
        )
        back_local = sum(
            response[lag][None, None, :] * grads_padded[:, lag : lag + P_SIZE]
            for lag in range(P_SIZE)
        )
        by_lag = jnp.stack(
            [
                jnp.sum(
                    blocks_padded[:, P_SIZE - 1 - lag : 2 * P_SIZE - 1 - lag] * some_grads,
                    axis=(0, 1),
                )
                for lag in range(P_SIZE)
            ],
            0,
        )
        local_terms = jnp.sum(by_lag[None] * decay_table, axis=1)
        return local_part, back_local, local_terms

    incoming, later_state, (local_part, back_local, local_terms) = entering(
        own_state, own_back, mode_rates, row_count, "ctx", (blocks, grad_blocks), local_work
    )

    gap = block_steps[:, None] - block_steps[None, :] - 1.0
    earlier = (gap >= 0).astype(jnp.float32)
    pair_decay = jnp.exp(
        -mode_rates[None, None] * (P_SIZE * jnp.maximum(gap, 0.0))[:, :, None, None]
    ) * earlier[:, :, None, None]
    starts = jnp.sum(pair_decay * block_ends[None], axis=1) + jnp.exp(
        -mode_rates[None] * (P_SIZE * block_steps)[:, None, None]
    ) * incoming[None]
    later_gap = block_steps[None, :] - block_steps[:, None] - 1.0
    later_mask = (later_gap >= 0).astype(jnp.float32)
    later_decay = jnp.exp(
        -mode_rates[None, None] * (P_SIZE * jnp.maximum(later_gap, 0.0))[:, :, None, None]
    ) * later_mask[:, :, None, None]
    ends_back = jnp.sum(later_decay * block_heads[None], axis=1) + jnp.exp(
        -mode_rates[None] * (P_SIZE * (block_count - 1 - block_steps))[:, None, None]
    ) * later_state[None]

    carried = jnp.sum(starts[:, :, None, :] * carried_table[None], axis=1)
    long_conv = (local_part + carried).reshape(row_count, chan_count)
    output = (query_part * long_conv).astype(jnp.bfloat16)
    grad_query = (cotangent * long_conv).astype(jnp.bfloat16)

    back_carried = jnp.sum(ends_back[:, :, None, :] * carried_reversed[None], axis=1)
    grad_product = (back_local + back_carried).reshape(row_count, chan_count)
    grad_key = (grad_product * value_part).astype(jnp.bfloat16)
    grad_value = (grad_product * key_part).astype(jnp.bfloat16)

    weighted = jnp.exp(-mode_rates)[None] * block_heads
    cross_part = jnp.sum(weighted * starts, axis=0)

    stacked_half = lax.optimization_barrier(jnp.stack([grad_query, grad_key, grad_value], 0))
    next_rows = passed_along(stacked_half[:, : KS - 1], "ctx", -1)
    stacked = stacked_half.astype(jnp.float32)
    after = jnp.concatenate([stacked, next_rows.astype(jnp.float32)], 1)
    grad_normed = sum(
        (
            short_filters[branch, offset][None, :] * after[branch, offset : offset + row_count]
            for branch in range(3)
            for offset in range(KS)
        )
    )
    short_terms = jnp.stack(
        [
            jnp.einsum(
                "btc,tc->bc",
                stacked_half,
                padded_half[KS - 1 - offset : KS - 1 - offset + row_count],
                preferred_element_type=jnp.float32,
            )
            for offset in range(KS)
        ],
        1,
    )
    partial_sums = jnp.concatenate(
        [cross_part + local_terms, short_terms.reshape(3 * KS, chan_count)], 0
    )
    whole_sums = summed(partial_sums, "ctx")
    norm_factor = 1.0 / jnp.sqrt(jnp.float32(total_rows))
    grad_residues = whole_sums[:M] * norm_factor
    grad_short = whole_sums[M:].reshape(3, KS, chan_count) * norm_factor
    row_dot = summed(jnp.sum(norm_gain[None, :] * grad_normed * stream_wide, axis=1), "ch")
    grad_stream = (
        row_scale[:, None] * norm_gain[None, :] * grad_normed
        - stream_wide * (row_scale**3 * row_dot / total_chans)[:, None]
    ).astype(jnp.bfloat16)
    return (output, grad_stream, grad_residues, grad_short)


def solution(mesh):
    devices = mesh.devices
    if all(hasattr(d, "coords") for d in devices.flat):
        coords = [tuple(d.coords) for d in devices.flat]
        PLACES["rings"] = tuple(max(c[k] for c in coords) + 1 for k in range(len(coords[0])))
        PLACES["ctx"] = [tuple(d.coords) for d in devices[:, 0]]
        PLACES["ch"] = [tuple(d.coords) for d in devices[0, :]]
    return jax.shard_map(
        per_device,
        mesh=mesh,
        in_specs=(
            P("ctx", "ch"),
            P("ch"),
            P(None, None, "ch"),
            P(None, "ch"),
            P(None, "ch"),
            P("ctx", "ch"),
        ),
        out_specs=(P("ctx", "ch"), P("ctx", "ch"), P(None, "ch"), P(None, None, "ch")),
        check_vma=False,
    )
```

```python
import jax
import jax.numpy as jnp
from jax import lax
from jax.sharding import PartitionSpec as P

M = 16
KS = 3
P_SIZE = 32


EPSILON = 1e-05


def passed_along(value, axis, steps):
    count = lax.axis_size(axis)
    first, last = (max(0, -steps), min(count, count - steps))
    return lax.ppermute(value, axis, [(source, source + steps) for source in range(first, last)])


def radices(count):
    levels = []
    while count > 1:
        radix = 4 if count % 4 == 0 else 2
        levels.append(radix)
        count //= radix
    return levels


PLACES = {}


def hops(first, second):
    rings = PLACES.get("rings")
    return sum(min(abs(a - b), ring - abs(a - b)) for a, b, ring in zip(first, second, rings))


def source_of(target, step, stride, radix, count, flip):
    digit = (target // stride) % radix
    position = (target % stride) ^ flip
    base = target - target % (stride * radix)
    return base + ((digit + step) % radix) * stride + position


def best_flip(axis, step, stride, radix, count):
    places = PLACES.get(axis)
    if places is None or len(places) != count:
        return 0
    best, flip_of_best = None, 0
    for flip in range(stride):
        far = [hops(places[source_of(t, step, stride, radix, count, flip)], places[t]) for t in range(count)]
        score = (max(far), sum(far))
        if best is None or score < best:
            best, flip_of_best = score, flip
    return flip_of_best


def members(value, axis, stride, radix):
    count = lax.axis_size(axis)
    digit = (lax.axis_index(axis) // stride) % radix
    received = [value]
    for step in range(1, radix):
        flip = best_flip(axis, step, stride, radix, count)
        pairs = [(source_of(t, step, stride, radix, count, flip), t) for t in range(count)]
        received.append(lax.ppermute(value, axis, pairs))
    ordered = [
        lax.select_n(((position - digit) % radix).astype(jnp.int32), *received)
        for position in range(radix)
    ]
    return ordered, digit


def power_of_two(count):
    return count & (count - 1) == 0


def entering(own_state, own_back, rates, rows, axis, riders):
    count = lax.axis_size(axis)
    place = lax.axis_index(axis)
    incoming = jnp.zeros_like(own_state)
    later = jnp.zeros_like(own_back)
    totals = jnp.stack([own_state, own_back], 0)
    stride = 1
    for radix in radices(count):
        group, digit = members(totals, axis, stride, radix)
        if stride == 1:
            group, riders = lax.optimization_barrier((group, riders))
        position = (place % stride).astype(jnp.float32)
        for other in range(radix):
            before = (digit > other).astype(jnp.float32)
            after = (digit < other).astype(jnp.float32)
            ahead = jnp.maximum(digit - 1 - other, 0).astype(jnp.float32) * stride + position
            behind = jnp.maximum(other - 1 - digit, 0).astype(jnp.float32) * stride + (
                stride - 1 - position
            )
            incoming = incoming + before * jnp.exp(-rates * (rows * ahead)) * group[other][0]
            later = later + after * jnp.exp(-rates * (rows * behind)) * group[other][1]
        forward_total = group[0][0]
        backward_total = group[0][1]
        for other in range(1, radix):
            forward_total = (
                jnp.exp(-rates * jnp.float32(rows * stride)) * forward_total + group[other][0]
            )
            backward_total = backward_total + jnp.exp(
                -rates * jnp.float32(rows * stride * other)
            ) * group[other][1]
        totals = jnp.stack([forward_total, backward_total], 0)
        stride *= radix
    return incoming, later, riders


def summed(value, axis):
    count = lax.axis_size(axis)
    if not power_of_two(count):
        return lax.psum(value, axis)
    stride = 1
    for radix in radices(count):
        group, _ = members(value, axis, stride, radix)
        if radix == 4:
            value = (group[0] + group[1]) + (group[2] + group[3])
        else:
            value = group[0] + group[1]
        stride *= radix
    return value


def summed_apart(first, second, axis):
    count = lax.axis_size(axis)
    levels = radices(count)
    if not power_of_two(count) or len(levels) < 2:
        return summed(first, axis), summed(second, axis)

    def level(value, stride, radix):
        group, _ = members(value, axis, stride, radix)
        if radix == 4:
            return (group[0] + group[1]) + (group[2] + group[3])
        return group[0] + group[1]

    first = level(first, 1, levels[0])
    second = level(second, 1, levels[0])
    value = jnp.concatenate([first, second], 0)
    stride = levels[0]
    for radix in levels[1:]:
        value = level(value, stride, radix)
        stride *= radix
    return value[: first.shape[0]], value[first.shape[0] :]


def per_device(stream, norm_gain, short_filters, mode_rates, residues, grad_out):
    row_count, chan_count = stream.shape
    block_count = row_count // P_SIZE
    total_chans = chan_count * lax.axis_size("ch")
    total_rows = row_count * lax.axis_size("ctx")
    stream_wide = stream.astype(jnp.float32)
    rim_rows = passed_along(stream[row_count - (KS - 1) :], "ctx", 1)
    with_rim = jnp.concatenate([rim_rows, stream], 0).astype(jnp.float32)
    squares = summed(jnp.sum(with_rim * with_rim, axis=1), "ch")
    scale_with_rim = lax.rsqrt(squares / total_chans + EPSILON)
    row_scale = scale_with_rim[KS - 1 :]
    padded_half = lax.optimization_barrier(
        (with_rim * scale_with_rim[:, None] * norm_gain[None, :]).astype(jnp.bfloat16)
    )
    padded = padded_half.astype(jnp.float32)
    branches = [
        sum(
            (
                short_filters[branch, offset][None, :]
                * padded[KS - 1 - offset : KS - 1 - offset + row_count]
                for offset in range(KS)
            )
        )
        for branch in range(3)
    ]
    query_part, key_part, value_part = branches
    product = lax.optimization_barrier((key_part * value_part).astype(jnp.bfloat16)).astype(
        jnp.float32
    )
    cotangent = grad_out.astype(jnp.float32)
    grad_conv = cotangent * query_part

    steps = jnp.arange(P_SIZE).astype(jnp.float32)
    decay_table = jnp.exp(-mode_rates[:, None, :] * steps[None, :, None])
    decay_reversed = jnp.exp(-mode_rates[:, None, :] * (P_SIZE - 1.0 - steps)[None, :, None])
    shifted = jnp.exp(-mode_rates[:, None, :] * (steps[None, :, None] + 1.0))
    response = jnp.sum(residues[:, None, :] * decay_table, axis=0)
    carried_table = shifted * residues[:, None, :]
    carried_reversed = (
        jnp.exp(-mode_rates[:, None, :] * (P_SIZE - steps)[None, :, None]) * residues[:, None, :]
    )

    blocks = product.reshape(block_count, P_SIZE, chan_count)
    grad_blocks = grad_conv.reshape(block_count, P_SIZE, chan_count)
    block_ends = jnp.sum(decay_reversed[None] * blocks[:, None], axis=2)
    block_heads = jnp.sum(decay_table[None] * grad_blocks[:, None], axis=2)
    block_steps = jnp.arange(block_count).astype(jnp.float32)
    own_state = jnp.sum(
        jnp.exp(-mode_rates[None] * (P_SIZE * (block_count - 1 - block_steps))[:, None, None])
        * block_ends,
        axis=0,
    )
    own_back = jnp.sum(
        jnp.exp(-mode_rates[None] * (P_SIZE * block_steps)[:, None, None]) * block_heads, axis=0
    )
    lead = jnp.zeros((block_count, P_SIZE - 1, chan_count), jnp.float32)
    incoming, later_state, (late_blocks, late_grads) = entering(
        own_state, own_back, mode_rates, row_count, "ctx", (blocks, grad_blocks)
    )
    late_padded = jnp.concatenate([lead, late_blocks], 1)

    gap = block_steps[:, None] - block_steps[None, :] - 1.0
    earlier = (gap >= 0).astype(jnp.float32)
    pair_decay = jnp.exp(
        -mode_rates[None, None] * (P_SIZE * jnp.maximum(gap, 0.0))[:, :, None, None]
    ) * earlier[:, :, None, None]
    starts = jnp.sum(pair_decay * block_ends[None], axis=1) + jnp.exp(
        -mode_rates[None] * (P_SIZE * block_steps)[:, None, None]
    ) * incoming[None]
    later_gap = block_steps[None, :] - block_steps[:, None] - 1.0
    later_mask = (later_gap >= 0).astype(jnp.float32)
    later_decay = jnp.exp(
        -mode_rates[None, None] * (P_SIZE * jnp.maximum(later_gap, 0.0))[:, :, None, None]
    ) * later_mask[:, :, None, None]
    ends_back = jnp.sum(later_decay * block_heads[None], axis=1) + jnp.exp(
        -mode_rates[None] * (P_SIZE * (block_count - 1 - block_steps))[:, None, None]
    ) * later_state[None]

    lead = jnp.zeros((block_count, P_SIZE - 1, chan_count), jnp.float32)
    blocks_padded = jnp.concatenate([lead, blocks], 1)
    grads_padded = jnp.concatenate([grad_blocks, lead], 1)
    local_part = sum(
        response[lag][None, None, :] * blocks_padded[:, P_SIZE - 1 - lag : 2 * P_SIZE - 1 - lag]
        for lag in range(P_SIZE)
    )
    carried = jnp.sum(starts[:, :, None, :] * carried_table[None], axis=1)
    long_conv = (local_part + carried).reshape(row_count, chan_count)
    output = (query_part * long_conv).astype(jnp.bfloat16)
    grad_query = (cotangent * long_conv).astype(jnp.bfloat16)

    back_local = sum(
        response[lag][None, None, :] * grads_padded[:, lag : lag + P_SIZE] for lag in range(P_SIZE)
    )
    back_carried = jnp.sum(ends_back[:, :, None, :] * carried_reversed[None], axis=1)
    grad_product = (back_local + back_carried).reshape(row_count, chan_count)
    grad_key = (grad_product * value_part).astype(jnp.bfloat16)
    grad_value = (grad_product * key_part).astype(jnp.bfloat16)

    weighted = jnp.exp(-mode_rates)[None] * block_heads
    cross_part = jnp.sum(weighted * starts, axis=0)
    by_lag = jnp.stack(
        [
            jnp.sum(
                late_padded[:, P_SIZE - 1 - lag : 2 * P_SIZE - 1 - lag] * late_grads, axis=(0, 1)
            )
            for lag in range(P_SIZE)
        ],
        0,
    )
    local_terms = jnp.sum(by_lag[None] * decay_table, axis=1)

    stacked_half = lax.optimization_barrier(jnp.stack([grad_query, grad_key, grad_value], 0))
    next_rows = passed_along(stacked_half[:, : KS - 1], "ctx", -1)
    stacked = stacked_half.astype(jnp.float32)
    after = jnp.concatenate([stacked, next_rows.astype(jnp.float32)], 1)
    grad_normed = sum(
        (
            short_filters[branch, offset][None, :] * after[branch, offset : offset + row_count]
            for branch in range(3)
            for offset in range(KS)
        )
    )
    short_terms = jnp.stack(
        [
            jnp.einsum(
                "btc,tc->bc",
                stacked_half,
                padded_half[KS - 1 - offset : KS - 1 - offset + row_count],
                preferred_element_type=jnp.float32,
            )
            for offset in range(KS)
        ],
        1,
    )
    residue_sum, short_sum = summed_apart(
        cross_part + local_terms, short_terms.reshape(3 * KS, chan_count), "ctx"
    )
    norm_factor = 1.0 / jnp.sqrt(jnp.float32(total_rows))
    grad_residues = residue_sum * norm_factor
    grad_short = short_sum.reshape(3, KS, chan_count) * norm_factor
    row_dot = summed(jnp.sum(norm_gain[None, :] * grad_normed * stream_wide, axis=1), "ch")
    grad_stream = (
        row_scale[:, None] * norm_gain[None, :] * grad_normed
        - stream_wide * (row_scale**3 * row_dot / total_chans)[:, None]
    ).astype(jnp.bfloat16)
    return (output, grad_stream, grad_residues, grad_short)


def solution(mesh):
    devices = mesh.devices
    if all(hasattr(d, "coords") for d in devices.flat):
        coords = [tuple(d.coords) for d in devices.flat]
        PLACES["rings"] = tuple(max(c[k] for c in coords) + 1 for k in range(len(coords[0])))
        PLACES["ctx"] = [tuple(d.coords) for d in devices[:, 0]]
        PLACES["ch"] = [tuple(d.coords) for d in devices[0, :]]
    return jax.shard_map(
        per_device,
        mesh=mesh,
        in_specs=(
            P("ctx", "ch"),
            P("ch"),
            P(None, None, "ch"),
            P(None, "ch"),
            P(None, "ch"),
            P("ctx", "ch"),
        ),
        out_specs=(P("ctx", "ch"), P("ctx", "ch"), P(None, "ch"), P(None, None, "ch")),
        check_vma=False,
    )
```

```python
import jax
import jax.numpy as jnp
from jax import lax
from jax.sharding import PartitionSpec as P

M = 16
KS = 3
P_SIZE = 32


EPSILON = 1e-05


def passed_along(value, axis, steps):
    count = lax.axis_size(axis)
    first, last = (max(0, -steps), min(count, count - steps))
    return lax.ppermute(value, axis, [(source, source + steps) for source in range(first, last)])


def radices(count):
    levels = []
    while count > 1:
        radix = 4 if count % 4 == 0 else 2
        levels.append(radix)
        count //= radix
    return levels


PLACES = {}


def hops(first, second):
    rings = PLACES.get("rings")
    return sum(min(abs(a - b), ring - abs(a - b)) for a, b, ring in zip(first, second, rings))


def source_of(target, step, stride, radix, count, flip):
    digit = (target // stride) % radix
    position = (target % stride) ^ flip
    base = target - target % (stride * radix)
    return base + ((digit + step) % radix) * stride + position


def best_flip(axis, step, stride, radix, count):
    places = PLACES.get(axis)
    if places is None or len(places) != count:
        return 0
    best, flip_of_best = None, 0
    for flip in range(stride):
        far = [hops(places[source_of(t, step, stride, radix, count, flip)], places[t]) for t in range(count)]
        score = (max(far), sum(far))
        if best is None or score < best:
            best, flip_of_best = score, flip
    return flip_of_best


def members(value, axis, stride, radix):
    count = lax.axis_size(axis)
    digit = (lax.axis_index(axis) // stride) % radix
    received = [value]
    for step in range(1, radix):
        flip = best_flip(axis, step, stride, radix, count)
        pairs = [(source_of(t, step, stride, radix, count, flip), t) for t in range(count)]
        received.append(lax.ppermute(value, axis, pairs))
    ordered = [
        lax.select_n(((position - digit) % radix).astype(jnp.int32), *received)
        for position in range(radix)
    ]
    return ordered, digit


def power_of_two(count):
    return count & (count - 1) == 0


def entering(own_state, own_back, rates, rows, axis, riders):
    count = lax.axis_size(axis)
    place = lax.axis_index(axis)
    incoming = jnp.zeros_like(own_state)
    later = jnp.zeros_like(own_back)
    totals = jnp.stack([own_state, own_back], 0)
    stride = 1
    for radix in radices(count):
        group, digit = members(totals, axis, stride, radix)
        if stride == 1:
            group, riders = lax.optimization_barrier((group, riders))
        position = (place % stride).astype(jnp.float32)
        for other in range(radix):
            before = (digit > other).astype(jnp.float32)
            after = (digit < other).astype(jnp.float32)
            ahead = jnp.maximum(digit - 1 - other, 0).astype(jnp.float32) * stride + position
            behind = jnp.maximum(other - 1 - digit, 0).astype(jnp.float32) * stride + (
                stride - 1 - position
            )
            incoming = incoming + before * jnp.exp(-rates * (rows * ahead)) * group[other][0]
            later = later + after * jnp.exp(-rates * (rows * behind)) * group[other][1]
        forward_total = group[0][0]
        backward_total = group[0][1]
        for other in range(1, radix):
            forward_total = (
                jnp.exp(-rates * jnp.float32(rows * stride)) * forward_total + group[other][0]
            )
            backward_total = backward_total + jnp.exp(
                -rates * jnp.float32(rows * stride * other)
            ) * group[other][1]
        totals = jnp.stack([forward_total, backward_total], 0)
        stride *= radix
    return incoming, later, riders


def summed(value, axis):
    count = lax.axis_size(axis)
    if not power_of_two(count):
        return lax.psum(value, axis)
    stride = 1
    for radix in radices(count):
        group, _ = members(value, axis, stride, radix)
        if radix == 4:
            value = (group[0] + group[1]) + (group[2] + group[3])
        else:
            value = group[0] + group[1]
        stride *= radix
    return value


def per_device(stream, norm_gain, short_filters, mode_rates, residues, grad_out):
    row_count, chan_count = stream.shape
    block_count = row_count // P_SIZE
    total_chans = chan_count * lax.axis_size("ch")
    total_rows = row_count * lax.axis_size("ctx")
    stream_wide = stream.astype(jnp.float32)
    rim_rows = passed_along(stream[row_count - (KS - 1) :], "ctx", 1)
    with_rim = jnp.concatenate([rim_rows, stream], 0).astype(jnp.float32)
    squares = summed(jnp.sum(with_rim * with_rim, axis=1), "ch")
    scale_with_rim = lax.rsqrt(squares / total_chans + EPSILON)
    row_scale = scale_with_rim[KS - 1 :]
    padded_half = lax.optimization_barrier(
        (with_rim * scale_with_rim[:, None] * norm_gain[None, :]).astype(jnp.bfloat16)
    )
    padded = padded_half.astype(jnp.float32)
    branches = [
        sum(
            (
                short_filters[branch, offset][None, :]
                * padded[KS - 1 - offset : KS - 1 - offset + row_count]
                for offset in range(KS)
            )
        )
        for branch in range(3)
    ]
    query_part, key_part, value_part = branches
    product = lax.optimization_barrier((key_part * value_part).astype(jnp.bfloat16)).astype(
        jnp.float32
    )
    cotangent = grad_out.astype(jnp.float32)
    grad_conv = cotangent * query_part

    steps = jnp.arange(P_SIZE).astype(jnp.float32)
    decay_table = jnp.exp(-mode_rates[:, None, :] * steps[None, :, None])
    decay_reversed = jnp.exp(-mode_rates[:, None, :] * (P_SIZE - 1.0 - steps)[None, :, None])
    shifted = jnp.exp(-mode_rates[:, None, :] * (steps[None, :, None] + 1.0))
    response = jnp.sum(residues[:, None, :] * decay_table, axis=0)
    carried_table = shifted * residues[:, None, :]
    carried_reversed = (
        jnp.exp(-mode_rates[:, None, :] * (P_SIZE - steps)[None, :, None]) * residues[:, None, :]
    )

    blocks = product.reshape(block_count, P_SIZE, chan_count)
    grad_blocks = grad_conv.reshape(block_count, P_SIZE, chan_count)
    block_ends = jnp.sum(decay_reversed[None] * blocks[:, None], axis=2)
    block_heads = jnp.sum(decay_table[None] * grad_blocks[:, None], axis=2)
    block_steps = jnp.arange(block_count).astype(jnp.float32)
    own_state = jnp.sum(
        jnp.exp(-mode_rates[None] * (P_SIZE * (block_count - 1 - block_steps))[:, None, None])
        * block_ends,
        axis=0,
    )
    own_back = jnp.sum(
        jnp.exp(-mode_rates[None] * (P_SIZE * block_steps)[:, None, None]) * block_heads, axis=0
    )
    lead = jnp.zeros((block_count, P_SIZE - 1, chan_count), jnp.float32)
    blocks_padded = jnp.concatenate([lead, blocks], 1)
    grads_padded = jnp.concatenate([grad_blocks, lead], 1)
    local_part = sum(
        response[lag][None, None, :] * blocks_padded[:, P_SIZE - 1 - lag : 2 * P_SIZE - 1 - lag]
        for lag in range(P_SIZE)
    )
    back_local = sum(
        response[lag][None, None, :] * grads_padded[:, lag : lag + P_SIZE] for lag in range(P_SIZE)
    )
    incoming, later_state, (late_blocks, late_grads, local_part, back_local) = entering(
        own_state, own_back, mode_rates, row_count, "ctx", (blocks, grad_blocks, local_part, back_local)
    )
    late_padded = jnp.concatenate([lead, late_blocks], 1)

    gap = block_steps[:, None] - block_steps[None, :] - 1.0
    earlier = (gap >= 0).astype(jnp.float32)
    pair_decay = jnp.exp(
        -mode_rates[None, None] * (P_SIZE * jnp.maximum(gap, 0.0))[:, :, None, None]
    ) * earlier[:, :, None, None]
    starts = jnp.sum(pair_decay * block_ends[None], axis=1) + jnp.exp(
        -mode_rates[None] * (P_SIZE * block_steps)[:, None, None]
    ) * incoming[None]
    later_gap = block_steps[None, :] - block_steps[:, None] - 1.0
    later_mask = (later_gap >= 0).astype(jnp.float32)
    later_decay = jnp.exp(
        -mode_rates[None, None] * (P_SIZE * jnp.maximum(later_gap, 0.0))[:, :, None, None]
    ) * later_mask[:, :, None, None]
    ends_back = jnp.sum(later_decay * block_heads[None], axis=1) + jnp.exp(
        -mode_rates[None] * (P_SIZE * (block_count - 1 - block_steps))[:, None, None]
    ) * later_state[None]

    carried = jnp.sum(starts[:, :, None, :] * carried_table[None], axis=1)
    long_conv = (local_part + carried).reshape(row_count, chan_count)
    output = (query_part * long_conv).astype(jnp.bfloat16)
    grad_query = (cotangent * long_conv).astype(jnp.bfloat16)

    back_carried = jnp.sum(ends_back[:, :, None, :] * carried_reversed[None], axis=1)
    grad_product = (back_local + back_carried).reshape(row_count, chan_count)
    grad_key = (grad_product * value_part).astype(jnp.bfloat16)
    grad_value = (grad_product * key_part).astype(jnp.bfloat16)

    weighted = jnp.exp(-mode_rates)[None] * block_heads
    cross_part = jnp.sum(weighted * starts, axis=0)
    by_lag = jnp.stack(
        [
            jnp.sum(
                late_padded[:, P_SIZE - 1 - lag : 2 * P_SIZE - 1 - lag] * late_grads, axis=(0, 1)
            )
            for lag in range(P_SIZE)
        ],
        0,
    )
    local_terms = jnp.sum(by_lag[None] * decay_table, axis=1)

    stacked_half = lax.optimization_barrier(jnp.stack([grad_query, grad_key, grad_value], 0))
    next_rows = passed_along(stacked_half[:, : KS - 1], "ctx", -1)
    stacked = stacked_half.astype(jnp.float32)
    after = jnp.concatenate([stacked, next_rows.astype(jnp.float32)], 1)
    grad_normed = sum(
        (
            short_filters[branch, offset][None, :] * after[branch, offset : offset + row_count]
            for branch in range(3)
            for offset in range(KS)
        )
    )
    short_terms = jnp.stack(
        [
            jnp.einsum(
                "btc,tc->bc",
                stacked_half,
                padded_half[KS - 1 - offset : KS - 1 - offset + row_count],
                preferred_element_type=jnp.float32,
            )
            for offset in range(KS)
        ],
        1,
    )
    partial_sums = jnp.concatenate(
        [cross_part + local_terms, short_terms.reshape(3 * KS, chan_count)], 0
    )
    whole_sums = summed(partial_sums, "ctx")
    norm_factor = 1.0 / jnp.sqrt(jnp.float32(total_rows))
    grad_residues = whole_sums[:M] * norm_factor
    grad_short = whole_sums[M:].reshape(3, KS, chan_count) * norm_factor
    row_dot = summed(jnp.sum(norm_gain[None, :] * grad_normed * stream_wide, axis=1), "ch")
    grad_stream = (
        row_scale[:, None] * norm_gain[None, :] * grad_normed
        - stream_wide * (row_scale**3 * row_dot / total_chans)[:, None]
    ).astype(jnp.bfloat16)
    return (output, grad_stream, grad_residues, grad_short)


def solution(mesh):
    devices = mesh.devices
    if all(hasattr(d, "coords") for d in devices.flat):
        coords = [tuple(d.coords) for d in devices.flat]
        PLACES["rings"] = tuple(max(c[k] for c in coords) + 1 for k in range(len(coords[0])))
        PLACES["ctx"] = [tuple(d.coords) for d in devices[:, 0]]
        PLACES["ch"] = [tuple(d.coords) for d in devices[0, :]]
    return jax.shard_map(
        per_device,
        mesh=mesh,
        in_specs=(
            P("ctx", "ch"),
            P("ch"),
            P(None, None, "ch"),
            P(None, "ch"),
            P(None, "ch"),
            P("ctx", "ch"),
        ),
        out_specs=(P("ctx", "ch"), P("ctx", "ch"), P(None, "ch"), P(None, None, "ch")),
        check_vma=False,
    )
```

```python
import jax
import jax.numpy as jnp
from jax import lax
from jax.sharding import PartitionSpec as P

M = 16
KS = 3
P_SIZE = 32


EPSILON = 1e-05


def passed_along(value, axis, steps):
    count = lax.axis_size(axis)
    first, last = (max(0, -steps), min(count, count - steps))
    return lax.ppermute(value, axis, [(source, source + steps) for source in range(first, last)])


def radices(count):
    levels = []
    while count > 1:
        radix = 4 if count % 4 == 0 else 2
        levels.append(radix)
        count //= radix
    return levels


PLACES = {}


def hops(first, second):
    rings = PLACES.get("rings")
    return sum(min(abs(a - b), ring - abs(a - b)) for a, b, ring in zip(first, second, rings))


def source_of(target, step, stride, radix, count, flip):
    digit = (target // stride) % radix
    position = (target % stride) ^ flip
    base = target - target % (stride * radix)
    return base + ((digit + step) % radix) * stride + position


def best_flip(axis, step, stride, radix, count):
    places = PLACES.get(axis)
    if places is None or len(places) != count:
        return 0
    best, flip_of_best = None, 0
    for flip in range(stride):
        far = [hops(places[source_of(t, step, stride, radix, count, flip)], places[t]) for t in range(count)]
        score = (max(far), sum(far))
        if best is None or score < best:
            best, flip_of_best = score, flip
    return flip_of_best


def members(value, axis, stride, radix):
    count = lax.axis_size(axis)
    digit = (lax.axis_index(axis) // stride) % radix
    received = [value]
    for step in range(1, radix):
        flip = best_flip(axis, step, stride, radix, count)
        pairs = [(source_of(t, step, stride, radix, count, flip), t) for t in range(count)]
        received.append(lax.ppermute(value, axis, pairs))
    ordered = [
        lax.select_n(((position - digit) % radix).astype(jnp.int32), *received)
        for position in range(radix)
    ]
    return ordered, digit


def power_of_two(count):
    return count & (count - 1) == 0


def entering(own_state, own_back, rates, rows, axis, riders):
    count = lax.axis_size(axis)
    place = lax.axis_index(axis)
    incoming = jnp.zeros_like(own_state)
    later = jnp.zeros_like(own_back)
    totals = jnp.stack([own_state, own_back], 0)
    stride = 1
    for radix in radices(count):
        group, digit = members(totals, axis, stride, radix)
        if stride == 1:
            group, riders = lax.optimization_barrier((group, riders))
        position = (place % stride).astype(jnp.float32)
        for other in range(radix):
            before = (digit > other).astype(jnp.float32)
            after = (digit < other).astype(jnp.float32)
            ahead = jnp.maximum(digit - 1 - other, 0).astype(jnp.float32) * stride + position
            behind = jnp.maximum(other - 1 - digit, 0).astype(jnp.float32) * stride + (
                stride - 1 - position
            )
            incoming = incoming + before * jnp.exp(-rates * (rows * ahead)) * group[other][0]
            later = later + after * jnp.exp(-rates * (rows * behind)) * group[other][1]
        forward_total = group[0][0]
        backward_total = group[0][1]
        for other in range(1, radix):
            forward_total = (
                jnp.exp(-rates * jnp.float32(rows * stride)) * forward_total + group[other][0]
            )
            backward_total = backward_total + jnp.exp(
                -rates * jnp.float32(rows * stride * other)
            ) * group[other][1]
        totals = jnp.stack([forward_total, backward_total], 0)
        stride *= radix
    return incoming, later, riders


def summed(value, axis):
    count = lax.axis_size(axis)
    if not power_of_two(count):
        return lax.psum(value, axis)
    stride = 1
    for radix in radices(count):
        group, _ = members(value, axis, stride, radix)
        if radix == 4:
            value = (group[0] + group[1]) + (group[2] + group[3])
        else:
            value = group[0] + group[1]
        stride *= radix
    return value


def per_device(stream, norm_gain, short_filters, mode_rates, residues, grad_out):
    row_count, chan_count = stream.shape
    block_count = row_count // P_SIZE
    total_chans = chan_count * lax.axis_size("ch")
    total_rows = row_count * lax.axis_size("ctx")
    stream_wide = stream.astype(jnp.float32)
    rim_rows = passed_along(stream[row_count - (KS - 1) :], "ctx", 1)
    with_rim = jnp.concatenate([rim_rows, stream], 0).astype(jnp.float32)
    squares = summed(jnp.sum(with_rim * with_rim, axis=1), "ch")
    scale_with_rim = lax.rsqrt(squares / total_chans + EPSILON)
    row_scale = scale_with_rim[KS - 1 :]
    padded_half = lax.optimization_barrier(
        (with_rim * scale_with_rim[:, None] * norm_gain[None, :]).astype(jnp.bfloat16)
    )
    padded = padded_half.astype(jnp.float32)
    branches = [
        sum(
            (
                short_filters[branch, offset][None, :]
                * padded[KS - 1 - offset : KS - 1 - offset + row_count]
                for offset in range(KS)
            )
        )
        for branch in range(3)
    ]
    query_part, key_part, value_part = branches
    product = lax.optimization_barrier((key_part * value_part).astype(jnp.bfloat16)).astype(
        jnp.float32
    )
    cotangent = grad_out.astype(jnp.float32)
    grad_conv = cotangent * query_part

    steps = jnp.arange(P_SIZE).astype(jnp.float32)
    decay_table = jnp.exp(-mode_rates[:, None, :] * steps[None, :, None])
    decay_reversed = jnp.exp(-mode_rates[:, None, :] * (P_SIZE - 1.0 - steps)[None, :, None])
    shifted = jnp.exp(-mode_rates[:, None, :] * (steps[None, :, None] + 1.0))
    response = jnp.sum(residues[:, None, :] * decay_table, axis=0)
    carried_table = shifted * residues[:, None, :]
    carried_reversed = (
        jnp.exp(-mode_rates[:, None, :] * (P_SIZE - steps)[None, :, None]) * residues[:, None, :]
    )

    blocks = product.reshape(block_count, P_SIZE, chan_count)
    grad_blocks = grad_conv.reshape(block_count, P_SIZE, chan_count)
    block_ends = jnp.sum(decay_reversed[None] * blocks[:, None], axis=2)
    block_heads = jnp.sum(decay_table[None] * grad_blocks[:, None], axis=2)
    block_steps = jnp.arange(block_count).astype(jnp.float32)
    own_state = jnp.sum(
        jnp.exp(-mode_rates[None] * (P_SIZE * (block_count - 1 - block_steps))[:, None, None])
        * block_ends,
        axis=0,
    )
    own_back = jnp.sum(
        jnp.exp(-mode_rates[None] * (P_SIZE * block_steps)[:, None, None]) * block_heads, axis=0
    )
    lead = jnp.zeros((block_count, P_SIZE - 1, chan_count), jnp.float32)
    incoming, later_state, (late_blocks, late_grads) = entering(
        own_state, own_back, mode_rates, row_count, "ctx", (blocks, grad_blocks)
    )
    late_padded = jnp.concatenate([lead, late_blocks], 1)

    gap = block_steps[:, None] - block_steps[None, :] - 1.0
    earlier = (gap >= 0).astype(jnp.float32)
    pair_decay = jnp.exp(
        -mode_rates[None, None] * (P_SIZE * jnp.maximum(gap, 0.0))[:, :, None, None]
    ) * earlier[:, :, None, None]
    starts = jnp.sum(pair_decay * block_ends[None], axis=1) + jnp.exp(
        -mode_rates[None] * (P_SIZE * block_steps)[:, None, None]
    ) * incoming[None]
    later_gap = block_steps[None, :] - block_steps[:, None] - 1.0
    later_mask = (later_gap >= 0).astype(jnp.float32)
    later_decay = jnp.exp(
        -mode_rates[None, None] * (P_SIZE * jnp.maximum(later_gap, 0.0))[:, :, None, None]
    ) * later_mask[:, :, None, None]
    ends_back = jnp.sum(later_decay * block_heads[None], axis=1) + jnp.exp(
        -mode_rates[None] * (P_SIZE * (block_count - 1 - block_steps))[:, None, None]
    ) * later_state[None]

    lead = jnp.zeros((block_count, P_SIZE - 1, chan_count), jnp.float32)
    blocks_padded = jnp.concatenate([lead, blocks], 1)
    grads_padded = jnp.concatenate([grad_blocks, lead], 1)
    local_part = sum(
        response[lag][None, None, :] * blocks_padded[:, P_SIZE - 1 - lag : 2 * P_SIZE - 1 - lag]
        for lag in range(P_SIZE)
    )
    carried = jnp.sum(starts[:, :, None, :] * carried_table[None], axis=1)
    long_conv = (local_part + carried).reshape(row_count, chan_count)
    output = (query_part * long_conv).astype(jnp.bfloat16)
    grad_query = (cotangent * long_conv).astype(jnp.bfloat16)

    back_local = sum(
        response[lag][None, None, :] * grads_padded[:, lag : lag + P_SIZE] for lag in range(P_SIZE)
    )
    back_carried = jnp.sum(ends_back[:, :, None, :] * carried_reversed[None], axis=1)
    grad_product = (back_local + back_carried).reshape(row_count, chan_count)
    grad_key = (grad_product * value_part).astype(jnp.bfloat16)
    grad_value = (grad_product * key_part).astype(jnp.bfloat16)

    weighted = jnp.exp(-mode_rates)[None] * block_heads
    cross_part = jnp.sum(weighted * starts, axis=0)
    by_lag = jnp.stack(
        [
            jnp.sum(
                late_padded[:, P_SIZE - 1 - lag : 2 * P_SIZE - 1 - lag] * late_grads, axis=(0, 1)
            )
            for lag in range(P_SIZE)
        ],
        0,
    )
    local_terms = jnp.sum(by_lag[None] * decay_table, axis=1)

    stacked_half = lax.optimization_barrier(jnp.stack([grad_query, grad_key, grad_value], 0))
    next_rows = passed_along(stacked_half[:, : KS - 1], "ctx", -1)
    stacked = stacked_half.astype(jnp.float32)
    after = jnp.concatenate([stacked, next_rows.astype(jnp.float32)], 1)
    grad_normed = sum(
        (
            short_filters[branch, offset][None, :] * after[branch, offset : offset + row_count]
            for branch in range(3)
            for offset in range(KS)
        )
    )
    short_terms = jnp.stack(
        [
            jnp.einsum(
                "btc,tc->bc",
                stacked_half,
                padded_half[KS - 1 - offset : KS - 1 - offset + row_count],
                preferred_element_type=jnp.float32,
            )
            for offset in range(KS)
        ],
        1,
    )
    partial_sums = jnp.concatenate(
        [cross_part + local_terms, short_terms.reshape(3 * KS, chan_count)], 0
    )
    norm_factor = 1.0 / jnp.sqrt(jnp.float32(total_rows))
    whole_sums = summed(partial_sums * norm_factor, "ctx")
    grad_residues = whole_sums[:M]
    grad_short = whole_sums[M:].reshape(3, KS, chan_count)
    row_dot = summed(jnp.sum(norm_gain[None, :] * grad_normed * stream_wide, axis=1), "ch")
    grad_stream = (
        row_scale[:, None] * norm_gain[None, :] * grad_normed
        - stream_wide * (row_scale**3 * row_dot / total_chans)[:, None]
    ).astype(jnp.bfloat16)
    return (output, grad_stream, grad_residues, grad_short)


def solution(mesh):
    devices = mesh.devices
    if all(hasattr(d, "coords") for d in devices.flat):
        coords = [tuple(d.coords) for d in devices.flat]
        PLACES["rings"] = tuple(max(c[k] for c in coords) + 1 for k in range(len(coords[0])))
        PLACES["ctx"] = [tuple(d.coords) for d in devices[:, 0]]
        PLACES["ch"] = [tuple(d.coords) for d in devices[0, :]]
    return jax.shard_map(
        per_device,
        mesh=mesh,
        in_specs=(
            P("ctx", "ch"),
            P("ch"),
            P(None, None, "ch"),
            P(None, "ch"),
            P(None, "ch"),
            P("ctx", "ch"),
        ),
        out_specs=(P("ctx", "ch"), P("ctx", "ch"), P(None, "ch"), P(None, None, "ch")),
        check_vma=False,
    )
```

```python
import jax
import jax.numpy as jnp
from jax import lax
from jax.sharding import PartitionSpec as P

M = 16
KS = 3
P_SIZE = 32


EPSILON = 1e-05


def passed_along(value, axis, steps):
    count = lax.axis_size(axis)
    first, last = (max(0, -steps), min(count, count - steps))
    return lax.ppermute(value, axis, [(source, source + steps) for source in range(first, last)])


def radices(count):
    levels = []
    while count > 1:
        radix = 4 if count % 4 == 0 else 2
        levels.append(radix)
        count //= radix
    return levels


PLACES = {}


def hops(first, second):
    rings = PLACES.get("rings")
    return sum(min(abs(a - b), ring - abs(a - b)) for a, b, ring in zip(first, second, rings))


def source_of(target, step, stride, radix, count, flip):
    digit = (target // stride) % radix
    position = (target % stride) ^ flip
    base = target - target % (stride * radix)
    return base + ((digit + step) % radix) * stride + position


def best_flip(axis, step, stride, radix, count):
    places = PLACES.get(axis)
    if places is None or len(places) != count:
        return 0
    best, flip_of_best = None, 0
    for flip in range(stride):
        far = [hops(places[source_of(t, step, stride, radix, count, flip)], places[t]) for t in range(count)]
        score = (max(far), sum(far))
        if best is None or score < best:
            best, flip_of_best = score, flip
    return flip_of_best


def members(value, axis, stride, radix):
    count = lax.axis_size(axis)
    digit = (lax.axis_index(axis) // stride) % radix
    received = [value]
    for step in range(1, radix):
        flip = best_flip(axis, step, stride, radix, count)
        pairs = [(source_of(t, step, stride, radix, count, flip), t) for t in range(count)]
        received.append(lax.ppermute(value, axis, pairs))
    ordered = [
        lax.select_n(((position - digit) % radix).astype(jnp.int32), *received)
        for position in range(radix)
    ]
    return ordered, digit


def power_of_two(count):
    return count & (count - 1) == 0


def entering(own_state, own_back, rates, rows, axis, riders):
    count = lax.axis_size(axis)
    place = lax.axis_index(axis)
    incoming = jnp.zeros_like(own_state)
    later = jnp.zeros_like(own_back)
    totals = jnp.stack([own_state, own_back], 0)
    stride = 1
    for radix in radices(count):
        group, digit = members(totals, axis, stride, radix)
        if stride == 1:
            group, riders = lax.optimization_barrier((group, riders))
        position = (place % stride).astype(jnp.float32)
        for other in range(radix):
            before = (digit > other).astype(jnp.float32)
            after = (digit < other).astype(jnp.float32)
            ahead = jnp.maximum(digit - 1 - other, 0).astype(jnp.float32) * stride + position
            behind = jnp.maximum(other - 1 - digit, 0).astype(jnp.float32) * stride + (
                stride - 1 - position
            )
            incoming = incoming + before * jnp.exp(-rates * (rows * ahead)) * group[other][0]
            later = later + after * jnp.exp(-rates * (rows * behind)) * group[other][1]
        forward_total = group[0][0]
        backward_total = group[0][1]
        for other in range(1, radix):
            forward_total = (
                jnp.exp(-rates * jnp.float32(rows * stride)) * forward_total + group[other][0]
            )
            backward_total = backward_total + jnp.exp(
                -rates * jnp.float32(rows * stride * other)
            ) * group[other][1]
        totals = jnp.stack([forward_total, backward_total], 0)
        stride *= radix
    return incoming, later, riders


def summed(value, axis, pairwise=False):
    count = lax.axis_size(axis)
    if not power_of_two(count):
        return lax.psum(value, axis)
    stride = 1
    for radix in [2] * (count.bit_length() - 1) if pairwise else radices(count):
        group, _ = members(value, axis, stride, radix)
        if radix == 4:
            value = (group[0] + group[1]) + (group[2] + group[3])
        else:
            value = group[0] + group[1]
        stride *= radix
    return value


def per_device(stream, norm_gain, short_filters, mode_rates, residues, grad_out):
    row_count, chan_count = stream.shape
    block_count = row_count // P_SIZE
    total_chans = chan_count * lax.axis_size("ch")
    total_rows = row_count * lax.axis_size("ctx")
    stream_wide = stream.astype(jnp.float32)
    rim_rows = passed_along(stream[row_count - (KS - 1) :], "ctx", 1)
    with_rim = jnp.concatenate([rim_rows, stream], 0).astype(jnp.float32)
    squares = summed(jnp.sum(with_rim * with_rim, axis=1), "ch")
    scale_with_rim = lax.rsqrt(squares / total_chans + EPSILON)
    row_scale = scale_with_rim[KS - 1 :]
    padded_half = lax.optimization_barrier(
        (with_rim * scale_with_rim[:, None] * norm_gain[None, :]).astype(jnp.bfloat16)
    )
    padded = padded_half.astype(jnp.float32)
    branches = [
        sum(
            (
                short_filters[branch, offset][None, :]
                * padded[KS - 1 - offset : KS - 1 - offset + row_count]
                for offset in range(KS)
            )
        )
        for branch in range(3)
    ]
    query_part, key_part, value_part = branches
    product = lax.optimization_barrier((key_part * value_part).astype(jnp.bfloat16)).astype(
        jnp.float32
    )
    cotangent = grad_out.astype(jnp.float32)
    grad_conv = cotangent * query_part

    steps = jnp.arange(P_SIZE).astype(jnp.float32)
    decay_table = jnp.exp(-mode_rates[:, None, :] * steps[None, :, None])
    decay_reversed = jnp.exp(-mode_rates[:, None, :] * (P_SIZE - 1.0 - steps)[None, :, None])
    shifted = jnp.exp(-mode_rates[:, None, :] * (steps[None, :, None] + 1.0))
    response = jnp.sum(residues[:, None, :] * decay_table, axis=0)
    carried_table = shifted * residues[:, None, :]
    carried_reversed = (
        jnp.exp(-mode_rates[:, None, :] * (P_SIZE - steps)[None, :, None]) * residues[:, None, :]
    )

    blocks = product.reshape(block_count, P_SIZE, chan_count)
    grad_blocks = grad_conv.reshape(block_count, P_SIZE, chan_count)
    block_ends = jnp.sum(decay_reversed[None] * blocks[:, None], axis=2)
    block_heads = jnp.sum(decay_table[None] * grad_blocks[:, None], axis=2)
    block_steps = jnp.arange(block_count).astype(jnp.float32)
    own_state = jnp.sum(
        jnp.exp(-mode_rates[None] * (P_SIZE * (block_count - 1 - block_steps))[:, None, None])
        * block_ends,
        axis=0,
    )
    own_back = jnp.sum(
        jnp.exp(-mode_rates[None] * (P_SIZE * block_steps)[:, None, None]) * block_heads, axis=0
    )
    lead = jnp.zeros((block_count, P_SIZE - 1, chan_count), jnp.float32)
    incoming, later_state, (late_blocks, late_grads) = entering(
        own_state, own_back, mode_rates, row_count, "ctx", (blocks, grad_blocks)
    )
    late_padded = jnp.concatenate([lead, late_blocks], 1)

    gap = block_steps[:, None] - block_steps[None, :] - 1.0
    earlier = (gap >= 0).astype(jnp.float32)
    pair_decay = jnp.exp(
        -mode_rates[None, None] * (P_SIZE * jnp.maximum(gap, 0.0))[:, :, None, None]
    ) * earlier[:, :, None, None]
    starts = jnp.sum(pair_decay * block_ends[None], axis=1) + jnp.exp(
        -mode_rates[None] * (P_SIZE * block_steps)[:, None, None]
    ) * incoming[None]
    later_gap = block_steps[None, :] - block_steps[:, None] - 1.0
    later_mask = (later_gap >= 0).astype(jnp.float32)
    later_decay = jnp.exp(
        -mode_rates[None, None] * (P_SIZE * jnp.maximum(later_gap, 0.0))[:, :, None, None]
    ) * later_mask[:, :, None, None]
    ends_back = jnp.sum(later_decay * block_heads[None], axis=1) + jnp.exp(
        -mode_rates[None] * (P_SIZE * (block_count - 1 - block_steps))[:, None, None]
    ) * later_state[None]

    lead = jnp.zeros((block_count, P_SIZE - 1, chan_count), jnp.float32)
    blocks_padded = jnp.concatenate([lead, blocks], 1)
    grads_padded = jnp.concatenate([grad_blocks, lead], 1)
    local_part = sum(
        response[lag][None, None, :] * blocks_padded[:, P_SIZE - 1 - lag : 2 * P_SIZE - 1 - lag]
        for lag in range(P_SIZE)
    )
    carried = jnp.sum(starts[:, :, None, :] * carried_table[None], axis=1)
    long_conv = (local_part + carried).reshape(row_count, chan_count)
    output = (query_part * long_conv).astype(jnp.bfloat16)
    grad_query = (cotangent * long_conv).astype(jnp.bfloat16)

    back_local = sum(
        response[lag][None, None, :] * grads_padded[:, lag : lag + P_SIZE] for lag in range(P_SIZE)
    )
    back_carried = jnp.sum(ends_back[:, :, None, :] * carried_reversed[None], axis=1)
    grad_product = (back_local + back_carried).reshape(row_count, chan_count)
    grad_key = (grad_product * value_part).astype(jnp.bfloat16)
    grad_value = (grad_product * key_part).astype(jnp.bfloat16)

    weighted = jnp.exp(-mode_rates)[None] * block_heads
    cross_part = jnp.sum(weighted * starts, axis=0)
    by_lag = jnp.stack(
        [
            jnp.sum(
                late_padded[:, P_SIZE - 1 - lag : 2 * P_SIZE - 1 - lag] * late_grads, axis=(0, 1)
            )
            for lag in range(P_SIZE)
        ],
        0,
    )
    local_terms = jnp.sum(by_lag[None] * decay_table, axis=1)

    stacked_half = lax.optimization_barrier(jnp.stack([grad_query, grad_key, grad_value], 0))
    next_rows = passed_along(stacked_half[:, : KS - 1], "ctx", -1)
    stacked = stacked_half.astype(jnp.float32)
    after = jnp.concatenate([stacked, next_rows.astype(jnp.float32)], 1)
    grad_normed = sum(
        (
            short_filters[branch, offset][None, :] * after[branch, offset : offset + row_count]
            for branch in range(3)
            for offset in range(KS)
        )
    )
    short_terms = jnp.stack(
        [
            jnp.einsum(
                "btc,tc->bc",
                stacked_half,
                padded_half[KS - 1 - offset : KS - 1 - offset + row_count],
                preferred_element_type=jnp.float32,
            )
            for offset in range(KS)
        ],
        1,
    )
    partial_sums = jnp.concatenate(
        [cross_part + local_terms, short_terms.reshape(3 * KS, chan_count)], 0
    )
    whole_sums = summed(partial_sums, "ctx")
    norm_factor = 1.0 / jnp.sqrt(jnp.float32(total_rows))
    grad_residues = whole_sums[:M] * norm_factor
    grad_short = whole_sums[M:].reshape(3, KS, chan_count) * norm_factor
    row_dot = summed(
        jnp.sum(norm_gain[None, :] * grad_normed * stream_wide, axis=1), "ch", pairwise=True
    )
    grad_stream = (
        row_scale[:, None] * norm_gain[None, :] * grad_normed
        - stream_wide * (row_scale**3 * row_dot / total_chans)[:, None]
    ).astype(jnp.bfloat16)
    return (output, grad_stream, grad_residues, grad_short)


def solution(mesh):
    devices = mesh.devices
    if all(hasattr(d, "coords") for d in devices.flat):
        coords = [tuple(d.coords) for d in devices.flat]
        PLACES["rings"] = tuple(max(c[k] for c in coords) + 1 for k in range(len(coords[0])))
        PLACES["ctx"] = [tuple(d.coords) for d in devices[:, 0]]
        PLACES["ch"] = [tuple(d.coords) for d in devices[0, :]]
    return jax.shard_map(
        per_device,
        mesh=mesh,
        in_specs=(
            P("ctx", "ch"),
            P("ch"),
            P(None, None, "ch"),
            P(None, "ch"),
            P(None, "ch"),
            P("ctx", "ch"),
        ),
        out_specs=(P("ctx", "ch"), P("ctx", "ch"), P(None, "ch"), P(None, None, "ch")),
        check_vma=False,
    )
```
